32 devices in a mesh: group: 2 (over y), ctx: 8 (over z, x), head: 2 (over core).
Axes of the slice: x: 2, y: 2, z: 4, core: 2. Of those that a mesh axis runs over, the one named last changes fastest.
Arguments:
- queries: bfloat16 [4096, 4096], P(('group', 'ctx'), 'head'), parts along dimension 0, may hold values from -7 to 7
- keys: bfloat16 [4096, 1024], P(('group', 'ctx'), 'head'), parts along dimension 0, may hold values from -4 to 4
- values: bfloat16 [4096, 1024], P(('group', 'ctx'), 'head'), parts along dimension 0, may hold values from -24 to 24
- doc_of_block: int32 [32], P('group'), parts along dimension 0, may hold values from 0 to 4, never falling along the last dimension, each value on 1 to 8 neighbouring positions
- out_weight: bfloat16 [4096, 4096], P('ctx', 'head'), may hold values from -0.09375 to 0.09375
Outputs:
- mixed: bfloat16 [4096, 4096], P(('group', 'ctx'), 'head'), parts along dimension 0
The draws below stay inside these ranges and needn't reach their ends.
There are 2 independent parts, one for each index of `group`. The reference program is written for one: setup_inputs(seed, part) draws one part's arguments, and reference() takes and returns one part's arrays. A program takes and returns all parts, laid end to end along the dimension named above; an argument that names none is the same for every part. Nothing has to cross between parts.
Inputs may be any that keep to these rules, and one draw needn't show every extreme that they name: `doc_of_block`: blocks of one document are consecutive, and a document covers at most 8 blocks.
All inputs are finite; a program needn't handle non-finite values.
Results may differ from the reference program's by a relative error of at most 0.006.
Values may be sent and summed in bfloat16 or wider, within the bound.
No kernel may reach another device: no remote copies, remote signals or barrier semaphores. Data moves between devices by JAX's collectives and lax.ppermute only.
A program may use at most 64 MiB of HBM per device.

```python
import math
import jax
import jax.numpy as jnp
import numpy as np
from jax import lax

D = 4096
QUERY_HEADS = 32
KEY_VALUE_HEADS = 8
HEAD_SIZE = 128
BLOCK_TOKENS = 128
PACKED_TOKENS = 2048
NBLK = 16
DOCB = 8
DOCS = 5


def draw_keys(key, part):
    local_shape = (PACKED_TOKENS, KEY_VALUE_HEADS * HEAD_SIZE)
    drawn = jnp.clip(jax.random.normal(jax.random.fold_in(key, 1), local_shape, jnp.float32), -4.0, 4.0)
    return drawn.astype(jnp.bfloat16)


def draw_queries(key, part):
    local_shape = (PACKED_TOKENS, QUERY_HEADS * HEAD_SIZE)
    drawn = jnp.clip(1.5 * jax.random.normal(jax.random.fold_in(key, 2), local_shape, jnp.float32), -7.0, 7.0)
    return drawn.astype(jnp.bfloat16)


def block_scale(own_key, extent, shards, least, top_value):
    loudness = 1.0
    for dim, shards_of in shards:
        steps = jax.random.uniform(jax.random.fold_in(jax.random.fold_in(own_key, 6), dim), (shards_of,), jnp.float32, least / len(shards), top_value / len(shards))
        loudness = loudness * jnp.repeat(jnp.exp(steps), extent[dim] // shards_of).reshape((-1,) + (1,) * (len(extent) - 1 - dim))
    return loudness


def split_up(count, total, most, lean):
    loads = [(1 << 20) // math.isqrt(grade ** lean) + 1 for grade in range(2, count + 1)]
    surplus, given = total - most - (count - 1), [1] * (count - 1)
    while surplus > 0:
        movable = [i for i in range(count - 1) if given[i] < most]
        pool, left = sum([loads[i] for i in movable]), surplus
        for i in movable:
            extra = min(most - given[i], max(1, left * loads[i] // pool), surplus)
            given[i] = given[i] + extra
            surplus = surplus - extra
    return np.array([most] + given)


def ragged_sizes(rng, count, total, most, skew):
    if count == 2:
        one = jax.random.randint(rng, (), max(1, total - most), min(most, total - 1) + 1)
        return jnp.stack([one, total - one])
    tallies = jnp.asarray(split_up(count, total, most, skew), jnp.int32)
    pairs = (count - 1) // 2
    source_of, sink = tallies[1:1 + 2 * pairs:2], tallies[2:2 + 2 * pairs:2]
    margin = jnp.minimum(source_of - 1, most - sink)
    passed = jax.random.randint(jax.random.fold_in(rng, 1), (pairs,), 0, 1 << 20) % (margin + 1)
    tallies = tallies.at[1:1 + 2 * pairs:2].set(source_of - passed).at[2:2 + 2 * pairs:2].set(sink + passed)
    return tallies[jax.random.permutation(jax.random.fold_in(rng, 2), count)]


def scatter_about(own_key, shape, width, reach, pieces=(), held_as=jnp.bfloat16):
    array = width * jax.random.normal(own_key, shape, jnp.float32)
    if pieces:
        array = array * block_scale(own_key, shape, pieces, -0.22, 0.18)
    return jnp.clip(array, -reach, reach).astype(held_as)


def setup_inputs(seed: int = 0, part: int = 0) -> dict:
    splits = jax.random.split(jax.random.key(seed), 6)
    own_keys = jax.random.split(jax.random.fold_in(splits[5], part), 6)
    queries = draw_queries(jax.random.fold_in(jax.random.fold_in(splits[5], part), 71), part)
    keys = draw_keys(jax.random.fold_in(jax.random.fold_in(splits[5], part), 71), part)
    values = scatter_about(own_keys[2], (PACKED_TOKENS, KEY_VALUE_HEADS * HEAD_SIZE), 4.0, 24.0, ((0, 8), (1, 2)))
    doc_of_block = jnp.searchsorted(jnp.cumsum(ragged_sizes(own_keys[3], DOCS, NBLK, DOCB, 2)), jnp.arange(NBLK), side="right").astype(jnp.int32)
    out_weight = scatter_about(splits[4], (QUERY_HEADS * HEAD_SIZE, D), (QUERY_HEADS * HEAD_SIZE) ** -0.5, 0.09375, ((0, 8), (1, 2)))
    return dict(queries=queries, keys=keys, values=values, doc_of_block=doc_of_block, out_weight=out_weight)


def reference(queries, keys, values, doc_of_block, out_weight):
    group_width = QUERY_HEADS // KEY_VALUE_HEADS
    score_scale = 1.0 / math.sqrt(HEAD_SIZE)
    same_doc = doc_of_block[:, None] == doc_of_block[None, :]
    first_block = jnp.argmax(same_doc, axis=1).astype(jnp.int32)
    offsets = jnp.arange(BLOCK_TOKENS, dtype=jnp.int32)

    def one_block(block_index):
        query_row_block = lax.dynamic_slice_in_dim(queries, block_index * BLOCK_TOKENS, BLOCK_TOKENS, 0)
        query_head_rows = query_row_block.astype(jnp.float32).reshape(BLOCK_TOKENS, KEY_VALUE_HEADS, group_width, HEAD_SIZE)
        query_pos = block_index * BLOCK_TOKENS + offsets

        def block_scores(key_block):
            key_row_block = lax.dynamic_slice_in_dim(keys, key_block * BLOCK_TOKENS, BLOCK_TOKENS, 0)
            key_head_rows = key_row_block.astype(jnp.float32).reshape(BLOCK_TOKENS, KEY_VALUE_HEADS, HEAD_SIZE)
            scores = jnp.einsum('qhgd,khd->hgqk', query_head_rows, key_head_rows) * score_scale
            key_pos = key_block * BLOCK_TOKENS + offsets
            causal = key_pos[None, :] <= query_pos[:, None]
            return jnp.where(causal, scores, -jnp.inf)

        def take_max(key_block, running_max):
            return jnp.maximum(running_max, lax.optimization_barrier(jnp.max(block_scores(key_block), axis=-1)))
        initial_maximum = jnp.full((KEY_VALUE_HEADS, group_width, BLOCK_TOKENS), -jnp.inf, dtype=jnp.float32)
        row_max = lax.fori_loop(first_block[block_index], block_index + 1, take_max, initial_maximum)

        def accumulate(key_block, state_now):
            summed, totals = state_now
            weights = jnp.exp(block_scores(key_block) - row_max[..., None])
            rounded = lax.optimization_barrier(weights.astype(jnp.bfloat16)).astype(jnp.float32)
            value_row_block = lax.dynamic_slice_in_dim(values, key_block * BLOCK_TOKENS, BLOCK_TOKENS, 0)
            value_head_rows = value_row_block.astype(jnp.float32).reshape(BLOCK_TOKENS, KEY_VALUE_HEADS, HEAD_SIZE)
            summed = summed + jnp.einsum('hgqk,khd->hgqd', rounded, value_head_rows)
            totals = totals + lax.optimization_barrier(jnp.sum(weights, axis=-1))
            return (summed, totals)
        initial_state = (jnp.zeros((KEY_VALUE_HEADS, group_width, BLOCK_TOKENS, HEAD_SIZE), jnp.float32), jnp.zeros((KEY_VALUE_HEADS, group_width, BLOCK_TOKENS), jnp.float32))
        summed, totals = lax.fori_loop(first_block[block_index], block_index + 1, accumulate, initial_state)
        attended = summed / totals[..., None]
        return jnp.transpose(attended, (2, 0, 1, 3)).reshape(BLOCK_TOKENS, QUERY_HEADS * HEAD_SIZE).astype(jnp.bfloat16)
    attended = lax.map(one_block, jnp.arange(NBLK, dtype=jnp.int32)).reshape(PACKED_TOKENS, QUERY_HEADS * HEAD_SIZE)
    return jnp.dot(attended, out_weight, preferred_element_type=jnp.float32).astype(jnp.bfloat16)
```

```python
import math

import jax
import jax.numpy as jnp
from jax import lax
from jax.sharding import PartitionSpec as P

HEAD_SIZE = 128
BLOCK_TOKENS = 128


def passed_along(array, axis, by):
    peers = lax.axis_size(axis)
    pairs = [(i, i + by) for i in range(peers) if 0 <= i + by < peers]
    return lax.ppermute(array, axis, pairs)


def lookup_docs(positions, doc_of_block):
    block_ids = jnp.floor_divide(positions, BLOCK_TOKENS)
    table_ids = jnp.arange(doc_of_block.shape[0], dtype=jnp.int32)
    matches = block_ids[:, None] == table_ids[None, :]
    return jnp.max(jnp.where(matches, doc_of_block[None, :], -1), axis=1)


def update(state_now, query_head_rows, key_piece, value_piece, visible):
    running_max, summed, totals = state_now
    rows_here = key_piece.shape[0]
    kv_heads = query_head_rows.shape[1]
    key_head_rows = key_piece.reshape(rows_here, kv_heads, HEAD_SIZE)
    value_head_rows = value_piece.reshape(rows_here, kv_heads, HEAD_SIZE)
    score_scale = 1.0 / math.sqrt(HEAD_SIZE)
    scores = (
        jnp.einsum(
            "qhgd,khd->hgqk", query_head_rows, key_head_rows, preferred_element_type=jnp.float32
        )
        * score_scale
    )
    scores = jnp.where(visible, scores, -1e30)
    new_max = jnp.maximum(running_max, jnp.max(scores, axis=-1))
    weights = jnp.where(visible, jnp.exp(scores - new_max[..., None]), 0.0)
    rescale = jnp.exp(running_max - new_max)
    products = jnp.einsum(
        "hgqk,khd->hgqd",
        weights.astype(jnp.bfloat16),
        value_head_rows,
        preferred_element_type=jnp.float32,
    )
    summed = summed * rescale[..., None] + products
    totals = totals * rescale + jnp.sum(weights, axis=-1)
    return (new_max, summed, totals)


def fresh_state(kv_heads, group_width, rows_here):
    return (
        jnp.full((kv_heads, group_width, rows_here), -1e30, jnp.float32),
        jnp.zeros((kv_heads, group_width, rows_here, HEAD_SIZE), jnp.float32),
        jnp.zeros((kv_heads, group_width, rows_here), jnp.float32),
    )


def finish(state_now, rows_here, q_heads):
    running_max, summed, totals = state_now
    attended = summed / totals[..., None]
    return (
        jnp.transpose(attended, (2, 0, 1, 3))
        .reshape(rows_here, q_heads * HEAD_SIZE)
        .astype(jnp.bfloat16)
    )


def per_device(queries, keys, values, doc_of_block, out_weight):
    tok_rows = queries.shape[0]
    kv_heads = keys.shape[1] // HEAD_SIZE
    q_heads = queries.shape[1] // HEAD_SIZE
    group_width = q_heads // kv_heads
    ctx_count = lax.axis_size("ctx")
    reach_devs = min(8, ctx_count // 2)
    ctx_index = lax.axis_index("ctx")
    query_start = ctx_index * tok_rows
    query_pos = query_start + jnp.arange(tok_rows, dtype=jnp.int32)
    query_doc = lookup_docs(query_pos, doc_of_block)
    query_head_rows = queries.reshape(tok_rows, kv_heads, group_width, HEAD_SIZE)

    def attend(state_now, key_piece, value_piece, key_start):
        key_pos = key_start + jnp.arange(key_piece.shape[0], dtype=jnp.int32)
        key_doc = lookup_docs(key_pos, doc_of_block)
        visible = (key_doc[None, :] == query_doc[:, None]) & (
            key_pos[None, :] <= query_pos[:, None]
        )
        return update(state_now, query_head_rows, key_piece, value_piece, visible)

    initial_state = fresh_state(kv_heads, group_width, tok_rows)
    state_now = attend(initial_state, keys, values, query_start)
    for distance in range(1, reach_devs + 1):
        prior_keys, prior_values = passed_along((keys, values), "ctx", distance)
        state_now = attend(state_now, prior_keys, prior_values, query_start - distance * tok_rows)
    attended = finish(state_now, tok_rows, q_heads)
    head_count = lax.axis_size("head")
    head_index = lax.axis_index("head")
    feature_rows = attended.shape[1]
    weight_rows = lax.all_gather(out_weight, "ctx", axis=0, tiled=True)

    def project(piece, source):
        rows = lax.dynamic_slice_in_dim(weight_rows, source * feature_rows, feature_rows, 0)
        return jnp.dot(piece, rows, preferred_element_type=jnp.float32)

    mixed = project(attended, head_index)
    for shift in range(1, head_count):
        pairs = [(i, (i + shift) % head_count) for i in range(head_count)]
        piece = lax.ppermute(attended, "head", pairs)
        mixed = mixed + project(piece, (head_index + head_count - shift) % head_count)
    return mixed.astype(jnp.bfloat16)


def solution(mesh):
    return jax.shard_map(
        per_device,
        mesh=mesh,
        in_specs=(
            P(("group", "ctx"), "head"),
            P(("group", "ctx"), "head"),
            P(("group", "ctx"), "head"),
            P("group"),
            P("ctx", "head"),
        ),
        out_specs=P(("group", "ctx"), "head"),
        check_vma=False,
    )
```

```python
import math

import jax
import jax.numpy as jnp
from jax import lax
from jax.sharding import PartitionSpec as P

HEAD_SIZE = 128
BLOCK_TOKENS = 128


def passed_along(array, axis, by):
    peers = lax.axis_size(axis)
    pairs = [(i, i + by) for i in range(peers) if 0 <= i + by < peers]
    return lax.ppermute(array, axis, pairs)


def lookup_docs(positions, doc_of_block):
    block_ids = jnp.floor_divide(positions, BLOCK_TOKENS)
    table_ids = jnp.arange(doc_of_block.shape[0], dtype=jnp.int32)
    matches = block_ids[:, None] == table_ids[None, :]
    return jnp.max(jnp.where(matches, doc_of_block[None, :], -1), axis=1)


def update(state_now, query_head_rows, key_piece, value_piece, visible):
    running_max, summed, totals = state_now
    rows_here = key_piece.shape[0]
    kv_heads = query_head_rows.shape[1]
    key_head_rows = key_piece.reshape(rows_here, kv_heads, HEAD_SIZE)
    value_head_rows = value_piece.reshape(rows_here, kv_heads, HEAD_SIZE)
    score_scale = 1.0 / math.sqrt(HEAD_SIZE)
    scores = (
        jnp.einsum(
            "qhgd,khd->hgqk", query_head_rows, key_head_rows, preferred_element_type=jnp.float32
        )
        * score_scale
    )
    scores = jnp.where(visible, scores, -1e30)
    new_max = jnp.maximum(running_max, jnp.max(scores, axis=-1))
    weights = jnp.where(visible, jnp.exp(scores - new_max[..., None]), 0.0)
    rescale = jnp.exp(running_max - new_max)
    products = jnp.einsum(
        "hgqk,khd->hgqd",
        weights.astype(jnp.bfloat16),
        value_head_rows,
        preferred_element_type=jnp.float32,
    )
    summed = summed * rescale[..., None] + products
    totals = totals * rescale + jnp.sum(weights, axis=-1)
    return (new_max, summed, totals)


def fresh_state(kv_heads, group_width, rows_here):
    return (
        jnp.full((kv_heads, group_width, rows_here), -1e30, jnp.float32),
        jnp.zeros((kv_heads, group_width, rows_here, HEAD_SIZE), jnp.float32),
        jnp.zeros((kv_heads, group_width, rows_here), jnp.float32),
    )


def finish(state_now, rows_here, q_heads):
    running_max, summed, totals = state_now
    attended = summed / totals[..., None]
    return (
        jnp.transpose(attended, (2, 0, 1, 3))
        .reshape(rows_here, q_heads * HEAD_SIZE)
        .astype(jnp.bfloat16)
    )


def head_features(attended):
    head_count = lax.axis_size("head")
    head_index = lax.axis_index("head")
    received = [attended]
    for shift in range(1, head_count):
        pairs = [(i, (i + shift) % head_count) for i in range(head_count)]
        received.append(lax.ppermute(attended, "head", pairs))
    pieces = []
    for source in range(head_count):
        shift_of = (head_index + head_count - source) % head_count
        piece = received[0]
        for shift in range(1, head_count):
            piece = jnp.where(shift_of == shift, received[shift], piece)
        pieces.append(piece)
    return jnp.concatenate(pieces, axis=1)


def ring_project(features, out_weight):
    count = lax.axis_size("ctx")
    order = [i for i in range(0, count, 2)] + sorted(range(1, count, 2), reverse=True)
    position_of = [0] * count
    for position, index in enumerate(order):
        position_of[index] = position
    ctx_index = lax.axis_index("ctx")
    position = jnp.asarray(position_of, jnp.int32)[ctx_index]
    order_table = jnp.asarray(order, jnp.int32)
    rows = out_weight.shape[0]

    def term(block, source):
        piece = lax.dynamic_slice_in_dim(features, source * rows, rows, 1)
        return jnp.dot(piece, block, preferred_element_type=jnp.float32)

    mixed = term(out_weight, ctx_index)
    ahead = [(order[p], order[(p + 1) % count]) for p in range(count)]
    behind = [(order[p], order[(p - 1) % count]) for p in range(count)]
    forward = backward = out_weight
    forward_steps = count // 2
    backward_steps = count - 1 - forward_steps
    for step in range(1, forward_steps + 1):
        forward = lax.ppermute(forward, "ctx", ahead)
        mixed = mixed + term(forward, order_table[(position + count - step) % count])
        if step <= backward_steps:
            backward = lax.ppermute(backward, "ctx", behind)
            mixed = mixed + term(backward, order_table[(position + step) % count])
    return mixed


def per_device(queries, keys, values, doc_of_block, out_weight):
    tok_rows = queries.shape[0]
    kv_heads = keys.shape[1] // HEAD_SIZE
    q_heads = queries.shape[1] // HEAD_SIZE
    group_width = q_heads // kv_heads
    ctx_count = lax.axis_size("ctx")
    reach_devs = min(8, ctx_count // 2)
    ctx_index = lax.axis_index("ctx")
    query_start = ctx_index * tok_rows
    query_pos = query_start + jnp.arange(tok_rows, dtype=jnp.int32)
    query_doc = lookup_docs(query_pos, doc_of_block)
    query_head_rows = queries.reshape(tok_rows, kv_heads, group_width, HEAD_SIZE)

    def attend(state_now, key_piece, value_piece, key_start):
        key_pos = key_start + jnp.arange(key_piece.shape[0], dtype=jnp.int32)
        key_doc = lookup_docs(key_pos, doc_of_block)
        visible = (key_doc[None, :] == query_doc[:, None]) & (
            key_pos[None, :] <= query_pos[:, None]
        )
        return update(state_now, query_head_rows, key_piece, value_piece, visible)

    initial_state = fresh_state(kv_heads, group_width, tok_rows)
    state_now = attend(initial_state, keys, values, query_start)
    for distance in range(1, reach_devs + 1):
        prior_keys, prior_values = passed_along((keys, values), "ctx", distance)
        state_now = attend(state_now, prior_keys, prior_values, query_start - distance * tok_rows)
    attended = finish(state_now, tok_rows, q_heads)
    features = head_features(attended)
    mixed = ring_project(features, out_weight)
    return mixed.astype(jnp.bfloat16)


def solution(mesh):
    return jax.shard_map(
        per_device,
        mesh=mesh,
        in_specs=(
            P(("group", "ctx"), "head"),
            P(("group", "ctx"), "head"),
            P(("group", "ctx"), "head"),
            P("group"),
            P("ctx", "head"),
        ),
        out_specs=P(("group", "ctx"), "head"),
        check_vma=False,
    )
```

```python
import math

import jax
import jax.numpy as jnp
from jax import lax
from jax.sharding import PartitionSpec as P

HEAD_SIZE = 128
BLOCK_TOKENS = 128


def passed_along(array, axis, by):
    peers = lax.axis_size(axis)
    pairs = [(i, i + by) for i in range(peers) if 0 <= i + by < peers]
    return lax.ppermute(array, axis, pairs)


def lookup_docs(positions, doc_of_block):
    block_ids = jnp.floor_divide(positions, BLOCK_TOKENS)
    table_ids = jnp.arange(doc_of_block.shape[0], dtype=jnp.int32)
    matches = block_ids[:, None] == table_ids[None, :]
    return jnp.max(jnp.where(matches, doc_of_block[None, :], -1), axis=1)


def update(state_now, query_head_rows, key_piece, value_piece, visible):
    running_max, summed, totals = state_now
    rows_here = key_piece.shape[0]
    kv_heads = query_head_rows.shape[1]
    key_head_rows = key_piece.reshape(rows_here, kv_heads, HEAD_SIZE)
    value_head_rows = value_piece.reshape(rows_here, kv_heads, HEAD_SIZE)
    score_scale = 1.0 / math.sqrt(HEAD_SIZE)
    scores = (
        jnp.einsum(
            "qhgd,khd->hgqk", query_head_rows, key_head_rows, preferred_element_type=jnp.float32
        )
        * score_scale
    )
    scores = jnp.where(visible, scores, -1e30)
    new_max = jnp.maximum(running_max, jnp.max(scores, axis=-1))
    weights = jnp.where(visible, jnp.exp(scores - new_max[..., None]), 0.0)
    rescale = jnp.exp(running_max - new_max)
    products = jnp.einsum(
        "hgqk,khd->hgqd",
        weights.astype(jnp.bfloat16),
        value_head_rows,
        preferred_element_type=jnp.float32,
    )
    summed = summed * rescale[..., None] + products
    totals = totals * rescale + jnp.sum(weights, axis=-1)
    return (new_max, summed, totals)


def fresh_state(kv_heads, group_width, rows_here):
    return (
        jnp.full((kv_heads, group_width, rows_here), -1e30, jnp.float32),
        jnp.zeros((kv_heads, group_width, rows_here, HEAD_SIZE), jnp.float32),
        jnp.zeros((kv_heads, group_width, rows_here), jnp.float32),
    )


def finish(state_now, rows_here, q_heads):
    running_max, summed, totals = state_now
    attended = summed / totals[..., None]
    return (
        jnp.transpose(attended, (2, 0, 1, 3))
        .reshape(rows_here, q_heads * HEAD_SIZE)
        .astype(jnp.bfloat16)
    )


def head_features(attended):
    head_count = lax.axis_size("head")
    head_index = lax.axis_index("head")
    received = [attended]
    for shift in range(1, head_count):
        pairs = [(i, (i + shift) % head_count) for i in range(head_count)]
        received.append(lax.ppermute(attended, "head", pairs))
    pieces = []
    for source in range(head_count):
        shift_of = (head_index + head_count - source) % head_count
        piece = received[0]
        for shift in range(1, head_count):
            piece = jnp.where(shift_of == shift, received[shift], piece)
        pieces.append(piece)
    return jnp.concatenate(pieces, axis=1)


def ring_project(features, out_weight):
    count = lax.axis_size("ctx")
    order = [i for i in range(0, count, 2)] + sorted(range(1, count, 2), reverse=True)
    position_of = [0] * count
    for position, index in enumerate(order):
        position_of[index] = position
    ctx_index = lax.axis_index("ctx")
    position = jnp.asarray(position_of, jnp.int32)[ctx_index]
    order_table = jnp.asarray(order, jnp.int32)
    rows = out_weight.shape[0]

    def term(block, source):
        piece = lax.dynamic_slice_in_dim(features, source * rows, rows, 1)
        return jnp.dot(piece, block, preferred_element_type=jnp.float32)

    mixed = term(out_weight, ctx_index)
    ahead = [(order[p], order[(p + 1) % count]) for p in range(count)]
    behind = [(order[p], order[(p - 1) % count]) for p in range(count)]
    forward = backward = out_weight
    forward_steps = count // 2
    backward_steps = count - 1 - forward_steps
    for step in range(1, forward_steps + 1):
        if step > backward_steps:
            half = out_weight.shape[1] // 2
            forward = lax.ppermute(forward[:, :half], "ctx", ahead)
            backward = lax.ppermute(backward[:, half:], "ctx", behind)
            joined = jnp.concatenate([forward, backward], axis=1)
            mixed = mixed + term(joined, order_table[(position + count - step) % count])
            break
        forward = lax.ppermute(forward, "ctx", ahead)
        mixed = mixed + term(forward, order_table[(position + count - step) % count])
        if step <= backward_steps:
            backward = lax.ppermute(backward, "ctx", behind)
            mixed = mixed + term(backward, order_table[(position + step) % count])
    return mixed


def per_device(queries, keys, values, doc_of_block, out_weight):
    tok_rows = queries.shape[0]
    kv_heads = keys.shape[1] // HEAD_SIZE
    q_heads = queries.shape[1] // HEAD_SIZE
    group_width = q_heads // kv_heads
    ctx_count = lax.axis_size("ctx")
    reach_devs = min(8, ctx_count // 2)
    ctx_index = lax.axis_index("ctx")
    query_start = ctx_index * tok_rows
    query_pos = query_start + jnp.arange(tok_rows, dtype=jnp.int32)
    query_doc = lookup_docs(query_pos, doc_of_block)
    query_head_rows = queries.reshape(tok_rows, kv_heads, group_width, HEAD_SIZE)

    def attend(state_now, key_piece, value_piece, key_start):
        key_pos = key_start + jnp.arange(key_piece.shape[0], dtype=jnp.int32)
        key_doc = lookup_docs(key_pos, doc_of_block)
        visible = (key_doc[None, :] == query_doc[:, None]) & (
            key_pos[None, :] <= query_pos[:, None]
        )
        return update(state_now, query_head_rows, key_piece, value_piece, visible)

    initial_state = fresh_state(kv_heads, group_width, tok_rows)
    state_now = attend(initial_state, keys, values, query_start)
    for distance in range(1, reach_devs + 1):
        prior_keys, prior_values = passed_along((keys, values), "ctx", distance)
        state_now = attend(state_now, prior_keys, prior_values, query_start - distance * tok_rows)
    attended = finish(state_now, tok_rows, q_heads)
    features = head_features(attended)
    mixed = ring_project(features, out_weight)
    return mixed.astype(jnp.bfloat16)


def solution(mesh):
    return jax.shard_map(
        per_device,
        mesh=mesh,
        in_specs=(
            P(("group", "ctx"), "head"),
            P(("group", "ctx"), "head"),
            P(("group", "ctx"), "head"),
            P("group"),
            P("ctx", "head"),
        ),
        out_specs=P(("group", "ctx"), "head"),
        check_vma=False,
    )
```

```python
import math

import jax
import jax.numpy as jnp
from jax import lax
from jax.sharding import PartitionSpec as P

HEAD_SIZE = 128
BLOCK_TOKENS = 128


def passed_along(array, axis, by):
    peers = lax.axis_size(axis)
    pairs = [(i, i + by) for i in range(peers) if 0 <= i + by < peers]
    return lax.ppermute(array, axis, pairs)


def lookup_docs(positions, doc_of_block):
    block_ids = jnp.floor_divide(positions, BLOCK_TOKENS)
    table_ids = jnp.arange(doc_of_block.shape[0], dtype=jnp.int32)
    matches = block_ids[:, None] == table_ids[None, :]
    return jnp.max(jnp.where(matches, doc_of_block[None, :], -1), axis=1)


def update(state_now, query_head_rows, key_piece, value_piece, visible):
    running_max, summed, totals = state_now
    rows_here = key_piece.shape[0]
    kv_heads = query_head_rows.shape[1]
    key_head_rows = key_piece.reshape(rows_here, kv_heads, HEAD_SIZE)
    value_head_rows = value_piece.reshape(rows_here, kv_heads, HEAD_SIZE)
    score_scale = 1.0 / math.sqrt(HEAD_SIZE)
    scores = (
        jnp.einsum(
            "qhgd,khd->hgqk", query_head_rows, key_head_rows, preferred_element_type=jnp.float32
        )
        * score_scale
    )
    scores = jnp.where(visible, scores, -1e30)
    new_max = jnp.maximum(running_max, jnp.max(scores, axis=-1))
    weights = jnp.where(visible, jnp.exp(scores - new_max[..., None]), 0.0)
    rescale = jnp.exp(running_max - new_max)
    products = jnp.einsum(
        "hgqk,khd->hgqd",
        weights.astype(jnp.bfloat16),
        value_head_rows,
        preferred_element_type=jnp.float32,
    )
    summed = summed * rescale[..., None] + products
    totals = totals * rescale + jnp.sum(weights, axis=-1)
    return (new_max, summed, totals)


def fresh_state(kv_heads, group_width, rows_here):
    return (
        jnp.full((kv_heads, group_width, rows_here), -1e30, jnp.float32),
        jnp.zeros((kv_heads, group_width, rows_here, HEAD_SIZE), jnp.float32),
        jnp.zeros((kv_heads, group_width, rows_here), jnp.float32),
    )


def finish(state_now, rows_here, q_heads):
    running_max, summed, totals = state_now
    attended = summed / totals[..., None]
    return (
        jnp.transpose(attended, (2, 0, 1, 3))
        .reshape(rows_here, q_heads * HEAD_SIZE)
        .astype(jnp.bfloat16)
    )


def head_features(attended):
    head_count = lax.axis_size("head")
    head_index = lax.axis_index("head")
    received = [attended]
    for shift in range(1, head_count):
        pairs = [(i, (i + shift) % head_count) for i in range(head_count)]
        received.append(lax.ppermute(attended, "head", pairs))
    pieces = []
    for source in range(head_count):
        shift_of = (head_index + head_count - source) % head_count
        piece = received[0]
        for shift in range(1, head_count):
            piece = jnp.where(shift_of == shift, received[shift], piece)
        pieces.append(piece)
    return jnp.concatenate(pieces, axis=1)


def ring_transfer(out_weight):
    count = lax.axis_size("ctx")
    order = list(range(0, count, 2)) + sorted(range(1, count, 2), reverse=True)
    position_of = [0] * count
    for position, index in enumerate(order):
        position_of[index] = position
    ctx_index = lax.axis_index("ctx")
    position = jnp.asarray(position_of, jnp.int32)[ctx_index]
    order_table = jnp.asarray(order, jnp.int32)
    columns = out_weight.shape[1]
    groups = lax.axis_size("group")
    group_index = lax.axis_index("group")
    own = (columns // 3) // 128 * 128 if groups == 2 else 0
    shared = columns - groups * own if own else columns
    swap = [(0, 1), (1, 0)]

    def carried(block):
        if not own:
            return block
        mine = lax.dynamic_slice_in_dim(block, shared + group_index * own, own, 1)
        return jnp.concatenate([block[:, :shared], mine], axis=1)

    def other_of(block):
        return lax.dynamic_slice_in_dim(block, shared + (1 - group_index) * own, own, 1)

    arrivals = [(ctx_index, carried(out_weight), other_of(out_weight) if own else None)]
    ahead = [(order[p], order[(p + 1) % count]) for p in range(count)]
    behind = [(order[p], order[(p - 1) % count]) for p in range(count)]
    forward = backward = carried(out_weight)
    forward_steps = count // 2
    backward_steps = count - 1 - forward_steps
    for step in range(1, forward_steps + 1):
        forward = lax.ppermute(forward, "ctx", ahead)
        crossed = lax.ppermute(forward[:, shared:], "group", swap) if own else None
        arrivals.append((order_table[(position + count - step) % count], forward, crossed))
        if step <= backward_steps:
            backward = lax.ppermute(backward, "ctx", behind)
            crossed = lax.ppermute(backward[:, shared:], "group", swap) if own else None
            arrivals.append((order_table[(position + step) % count], backward, crossed))
    return arrivals, shared, own


def ring_project(features, arrivals, shared, own, rows):
    group_index = lax.axis_index("group")
    parts = None
    for source, carried_block, crossed in arrivals:
        piece = lax.dynamic_slice_in_dim(features, source * rows, rows, 1)
        terms = [jnp.dot(piece, carried_block, preferred_element_type=jnp.float32)]
        if own:
            terms.append(jnp.dot(piece, crossed, preferred_element_type=jnp.float32))
        parts = terms if parts is None else [a + b for a, b in zip(parts, terms)]
    if not own:
        return parts[0]
    mine, other = parts[0][:, shared:], parts[1]
    first = jnp.where(group_index == 0, mine, other)
    second = jnp.where(group_index == 0, other, mine)
    return jnp.concatenate([parts[0][:, :shared], first, second], axis=1)

def per_device(queries, keys, values, doc_of_block, out_weight):
    tok_rows = queries.shape[0]
    kv_heads = keys.shape[1] // HEAD_SIZE
    q_heads = queries.shape[1] // HEAD_SIZE
    group_width = q_heads // kv_heads
    ctx_count = lax.axis_size("ctx")
    reach_devs = min(8, ctx_count // 2)
    ctx_index = lax.axis_index("ctx")
    query_start = ctx_index * tok_rows
    query_pos = query_start + jnp.arange(tok_rows, dtype=jnp.int32)
    query_doc = lookup_docs(query_pos, doc_of_block)
    query_head_rows = queries.reshape(tok_rows, kv_heads, group_width, HEAD_SIZE)

    def attend(state_now, key_piece, value_piece, key_start):
        key_pos = key_start + jnp.arange(key_piece.shape[0], dtype=jnp.int32)
        key_doc = lookup_docs(key_pos, doc_of_block)
        visible = (key_doc[None, :] == query_doc[:, None]) & (
            key_pos[None, :] <= query_pos[:, None]
        )
        return update(state_now, query_head_rows, key_piece, value_piece, visible)

    arrivals, shared, own = ring_transfer(out_weight)
    initial_state = fresh_state(kv_heads, group_width, tok_rows)
    state_now = attend(initial_state, keys, values, query_start)
    for distance in range(1, reach_devs + 1):
        prior_keys, prior_values = passed_along((keys, values), "ctx", distance)
        state_now = attend(state_now, prior_keys, prior_values, query_start - distance * tok_rows)
    attended = finish(state_now, tok_rows, q_heads)
    features = head_features(attended)
    mixed = ring_project(features, arrivals, shared, own, out_weight.shape[0])
    return mixed.astype(jnp.bfloat16)


def solution(mesh):
    return jax.shard_map(
        per_device,
        mesh=mesh,
        in_specs=(
            P(("group", "ctx"), "head"),
            P(("group", "ctx"), "head"),
            P(("group", "ctx"), "head"),
            P("group"),
            P("ctx", "head"),
        ),
        out_specs=P(("group", "ctx"), "head"),
        check_vma=False,
    )
```

```python
import math

import jax
import jax.numpy as jnp
from jax import lax
from jax.sharding import PartitionSpec as P

HEAD_SIZE = 128
BLOCK_TOKENS = 128


def passed_along(array, axis, by):
    peers = lax.axis_size(axis)
    pairs = [(i, i + by) for i in range(peers) if 0 <= i + by < peers]
    return lax.ppermute(array, axis, pairs)


def lookup_docs(positions, doc_of_block):
    block_ids = jnp.floor_divide(positions, BLOCK_TOKENS)
    table_ids = jnp.arange(doc_of_block.shape[0], dtype=jnp.int32)
    matches = block_ids[:, None] == table_ids[None, :]
    return jnp.max(jnp.where(matches, doc_of_block[None, :], -1), axis=1)


def update(state_now, query_head_rows, key_piece, value_piece, visible):
    running_max, summed, totals = state_now
    rows_here = key_piece.shape[0]
    kv_heads = query_head_rows.shape[1]
    key_head_rows = key_piece.reshape(rows_here, kv_heads, HEAD_SIZE)
    value_head_rows = value_piece.reshape(rows_here, kv_heads, HEAD_SIZE)
    score_scale = 1.0 / math.sqrt(HEAD_SIZE)
    scores = (
        jnp.einsum(
            "qhgd,khd->hgqk", query_head_rows, key_head_rows, preferred_element_type=jnp.float32
        )
        * score_scale
    )
    scores = jnp.where(visible, scores, -1e30)
    new_max = jnp.maximum(running_max, jnp.max(scores, axis=-1))
    weights = jnp.where(visible, jnp.exp(scores - new_max[..., None]), 0.0)
    rescale = jnp.exp(running_max - new_max)
    products = jnp.einsum(
        "hgqk,khd->hgqd",
        weights.astype(jnp.bfloat16),
        value_head_rows,
        preferred_element_type=jnp.float32,
    )
    summed = summed * rescale[..., None] + products
    totals = totals * rescale + jnp.sum(weights, axis=-1)
    return (new_max, summed, totals)


def fresh_state(kv_heads, group_width, rows_here):
    return (
        jnp.full((kv_heads, group_width, rows_here), -1e30, jnp.float32),
        jnp.zeros((kv_heads, group_width, rows_here, HEAD_SIZE), jnp.float32),
        jnp.zeros((kv_heads, group_width, rows_here), jnp.float32),
    )


def finish(state_now, rows_here, q_heads):
    running_max, summed, totals = state_now
    attended = summed / totals[..., None]
    return (
        jnp.transpose(attended, (2, 0, 1, 3))
        .reshape(rows_here, q_heads * HEAD_SIZE)
        .astype(jnp.bfloat16)
    )


def head_features(attended):
    head_count = lax.axis_size("head")
    head_index = lax.axis_index("head")
    received = [attended]
    for shift in range(1, head_count):
        pairs = [(i, (i + shift) % head_count) for i in range(head_count)]
        received.append(lax.ppermute(attended, "head", pairs))
    pieces = []
    for source in range(head_count):
        shift_of = (head_index + head_count - source) % head_count
        piece = received[0]
        for shift in range(1, head_count):
            piece = jnp.where(shift_of == shift, received[shift], piece)
        pieces.append(piece)
    return jnp.concatenate(pieces, axis=1)


def ring_transfer(out_weight):
    count = lax.axis_size("ctx")
    order = list(range(0, count, 2)) + sorted(range(1, count, 2), reverse=True)
    position_of = [0] * count
    for position, index in enumerate(order):
        position_of[index] = position
    ctx_index = lax.axis_index("ctx")
    position = jnp.asarray(position_of, jnp.int32)[ctx_index]
    order_table = jnp.asarray(order, jnp.int32)
    columns = out_weight.shape[1]
    groups = lax.axis_size("group")
    group_index = lax.axis_index("group")
    own = (columns // 3) // 128 * 128 if groups == 2 else 0
    shared = columns - groups * own if own else columns
    swap = [(0, 1), (1, 0)]

    def carried(block):
        if not own:
            return block
        mine = lax.dynamic_slice_in_dim(block, shared + group_index * own, own, 1)
        return jnp.concatenate([block[:, :shared], mine], axis=1)

    def other_of(block):
        return lax.dynamic_slice_in_dim(block, shared + (1 - group_index) * own, own, 1)

    arrivals = [(ctx_index, carried(out_weight), other_of(out_weight) if own else None)]
    ahead = [(order[p], order[(p + 1) % count]) for p in range(count)]
    behind = [(order[p], order[(p - 1) % count]) for p in range(count)]
    forward = backward = carried(out_weight)
    forward_steps = count // 2
    backward_steps = count - 1 - forward_steps
    for step in range(1, forward_steps + 1):
        forward = lax.ppermute(forward, "ctx", ahead)
        crossed = lax.ppermute(forward[:, shared:], "group", swap) if own else None
        arrivals.append((order_table[(position + count - step) % count], forward, crossed))
        if step <= backward_steps:
            backward = lax.ppermute(backward, "ctx", behind)
            crossed = lax.ppermute(backward[:, shared:], "group", swap) if own else None
            arrivals.append((order_table[(position + step) % count], backward, crossed))
    return arrivals, shared, own


def ring_project(features, arrivals, shared, own, rows):
    group_index = lax.axis_index("group")
    parts = None
    for source, carried_block, crossed in arrivals:
        piece = lax.dynamic_slice_in_dim(features, source * rows, rows, 1)
        terms = [jnp.dot(piece, carried_block, preferred_element_type=jnp.float32)]
        if own:
            terms.append(jnp.dot(piece, crossed, preferred_element_type=jnp.float32))
        parts = terms if parts is None else [a + b for a, b in zip(parts, terms)]
    if not own:
        return parts[0]
    mine, other = parts[0][:, shared:], parts[1]
    first = jnp.where(group_index == 0, mine, other)
    second = jnp.where(group_index == 0, other, mine)
    return jnp.concatenate([parts[0][:, :shared], first, second], axis=1)

def per_device(queries, keys, values, doc_of_block, out_weight):
    tok_rows = queries.shape[0]
    kv_heads = keys.shape[1] // HEAD_SIZE
    q_heads = queries.shape[1] // HEAD_SIZE
    group_width = q_heads // kv_heads
    ctx_count = lax.axis_size("ctx")
    reach_devs = min(8, ctx_count // 2)
    ctx_index = lax.axis_index("ctx")
    query_start = ctx_index * tok_rows
    query_pos = query_start + jnp.arange(tok_rows, dtype=jnp.int32)
    query_doc = lookup_docs(query_pos, doc_of_block)
    query_head_rows = queries.reshape(tok_rows, kv_heads, group_width, HEAD_SIZE)

    def attend(state_now, key_piece, value_piece, key_start):
        key_pos = key_start + jnp.arange(key_piece.shape[0], dtype=jnp.int32)
        key_doc = lookup_docs(key_pos, doc_of_block)
        visible = (key_doc[None, :] == query_doc[:, None]) & (
            key_pos[None, :] <= query_pos[:, None]
        )
        return update(state_now, query_head_rows, key_piece, value_piece, visible)

    arrivals, shared, own = ring_transfer(out_weight)
    initial_state = fresh_state(kv_heads, group_width, tok_rows)
    state_now = attend(initial_state, keys, values, query_start)
    first_block = arrivals[1][1]
    first_block, keys, values = lax.optimization_barrier((first_block, keys, values))
    arrivals[1] = (arrivals[1][0], first_block, arrivals[1][2])
    for distance in range(1, reach_devs + 1):
        prior_keys, prior_values = passed_along((keys, values), "ctx", distance)
        state_now = attend(state_now, prior_keys, prior_values, query_start - distance * tok_rows)
    attended = finish(state_now, tok_rows, q_heads)
    features = head_features(attended)
    mixed = ring_project(features, arrivals, shared, own, out_weight.shape[0])
    return mixed.astype(jnp.bfloat16)


def solution(mesh):
    return jax.shard_map(
        per_device,
        mesh=mesh,
        in_specs=(
            P(("group", "ctx"), "head"),
            P(("group", "ctx"), "head"),
            P(("group", "ctx"), "head"),
            P("group"),
            P("ctx", "head"),
        ),
        out_specs=P(("group", "ctx"), "head"),
        check_vma=False,
    )
```

```python
import math

import jax
import jax.numpy as jnp
from jax import lax
from jax.sharding import PartitionSpec as P

HEAD_SIZE = 128
BLOCK_TOKENS = 128


def passed_along(array, axis, by):
    peers = lax.axis_size(axis)
    pairs = [(i, i + by) for i in range(peers) if 0 <= i + by < peers]
    return lax.ppermute(array, axis, pairs)


def lookup_docs(positions, doc_of_block):
    block_ids = jnp.floor_divide(positions, BLOCK_TOKENS)
    table_ids = jnp.arange(doc_of_block.shape[0], dtype=jnp.int32)
    matches = block_ids[:, None] == table_ids[None, :]
    return jnp.max(jnp.where(matches, doc_of_block[None, :], -1), axis=1)


def update(state_now, query_head_rows, key_piece, value_piece, visible):
    running_max, summed, totals = state_now
    rows_here = key_piece.shape[0]
    kv_heads = query_head_rows.shape[1]
    key_head_rows = key_piece.reshape(rows_here, kv_heads, HEAD_SIZE)
    value_head_rows = value_piece.reshape(rows_here, kv_heads, HEAD_SIZE)
    score_scale = 1.0 / math.sqrt(HEAD_SIZE)
    scores = (
        jnp.einsum(
            "qhgd,khd->hgqk", query_head_rows, key_head_rows, preferred_element_type=jnp.float32
        )
        * score_scale
    )
    scores = jnp.where(visible, scores, -1e30)
    new_max = jnp.maximum(running_max, jnp.max(scores, axis=-1))
    weights = jnp.where(visible, jnp.exp(scores - new_max[..., None]), 0.0)
    rescale = jnp.exp(running_max - new_max)
    products = jnp.einsum(
        "hgqk,khd->hgqd",
        weights.astype(jnp.bfloat16),
        value_head_rows,
        preferred_element_type=jnp.float32,
    )
    summed = summed * rescale[..., None] + products
    totals = totals * rescale + jnp.sum(weights, axis=-1)
    return (new_max, summed, totals)


def fresh_state(kv_heads, group_width, rows_here):
    return (
        jnp.full((kv_heads, group_width, rows_here), -1e30, jnp.float32),
        jnp.zeros((kv_heads, group_width, rows_here, HEAD_SIZE), jnp.float32),
        jnp.zeros((kv_heads, group_width, rows_here), jnp.float32),
    )


def finish(state_now, rows_here, q_heads):
    running_max, summed, totals = state_now
    attended = summed / totals[..., None]
    return (
        jnp.transpose(attended, (2, 0, 1, 3))
        .reshape(rows_here, q_heads * HEAD_SIZE)
        .astype(jnp.bfloat16)
    )


def head_features(attended):
    head_count = lax.axis_size("head")
    head_index = lax.axis_index("head")
    received = [attended]
    for shift in range(1, head_count):
        pairs = [(i, (i + shift) % head_count) for i in range(head_count)]
        received.append(lax.ppermute(attended, "head", pairs))
    pieces = []
    for source in range(head_count):
        shift_of = (head_index + head_count - source) % head_count
        piece = received[0]
        for shift in range(1, head_count):
            piece = jnp.where(shift_of == shift, received[shift], piece)
        pieces.append(piece)
    return jnp.concatenate(pieces, axis=1)


def ring_transfer(out_weight):
    count = lax.axis_size("ctx")
    order = list(range(0, count, 2)) + sorted(range(1, count, 2), reverse=True)
    position_of = [0] * count
    for position, index in enumerate(order):
        position_of[index] = position
    ctx_index = lax.axis_index("ctx")
    position = jnp.asarray(position_of, jnp.int32)[ctx_index]
    order_table = jnp.asarray(order, jnp.int32)
    columns = out_weight.shape[1]
    groups = lax.axis_size("group")
    group_index = lax.axis_index("group")
    own = (columns // 3) // 128 * 128 if groups == 2 else 0
    shared = columns - groups * own if own else columns
    swap = [(0, 1), (1, 0)]

    def carried(block):
        if not own:
            return block
        mine = lax.dynamic_slice_in_dim(block, shared + group_index * own, own, 1)
        return jnp.concatenate([block[:, :shared], mine], axis=1)

    def other_of(block):
        return lax.dynamic_slice_in_dim(block, shared + (1 - group_index) * own, own, 1)

    arrivals = [(ctx_index, carried(out_weight), other_of(out_weight) if own else None)]
    ahead = [(order[p], order[(p + 1) % count]) for p in range(count)]
    behind = [(order[p], order[(p - 1) % count]) for p in range(count)]
    forward = backward = carried(out_weight)
    forward_steps = count // 2
    backward_steps = count - 1 - forward_steps
    for step in range(1, forward_steps + 1):
        forward = lax.ppermute(forward, "ctx", ahead)
        crossed = lax.ppermute(forward[:, shared:], "group", swap) if own else None
        arrivals.append((order_table[(position + count - step) % count], forward, crossed))
        if step <= backward_steps:
            backward = lax.ppermute(backward, "ctx", behind)
            crossed = lax.ppermute(backward[:, shared:], "group", swap) if own else None
            arrivals.append((order_table[(position + step) % count], backward, crossed))
    return arrivals, shared, own


def ring_project(features, arrivals, shared, own, rows):
    group_index = lax.axis_index("group")
    parts = None
    for source, carried_block, crossed in arrivals:
        piece = lax.dynamic_slice_in_dim(features, source * rows, rows, 1)
        terms = [jnp.dot(piece, carried_block, preferred_element_type=jnp.float32)]
        if own:
            terms.append(jnp.dot(piece, crossed, preferred_element_type=jnp.float32))
        parts = terms if parts is None else [a + b for a, b in zip(parts, terms)]
    if not own:
        return parts[0]
    mine, other = parts[0][:, shared:], parts[1]
    first = jnp.where(group_index == 0, mine, other)
    second = jnp.where(group_index == 0, other, mine)
    return jnp.concatenate([parts[0][:, :shared], first, second], axis=1)

def per_device(queries, keys, values, doc_of_block, out_weight):
    tok_rows = queries.shape[0]
    kv_heads = keys.shape[1] // HEAD_SIZE
    q_heads = queries.shape[1] // HEAD_SIZE
    group_width = q_heads // kv_heads
    ctx_count = lax.axis_size("ctx")
    reach_devs = min(8, ctx_count // 2)
    ctx_index = lax.axis_index("ctx")
    query_start = ctx_index * tok_rows
    query_pos = query_start + jnp.arange(tok_rows, dtype=jnp.int32)
    query_doc = lookup_docs(query_pos, doc_of_block)
    query_head_rows = queries.reshape(tok_rows, kv_heads, group_width, HEAD_SIZE)

    def attend(state_now, key_piece, value_piece, key_start):
        key_pos = key_start + jnp.arange(key_piece.shape[0], dtype=jnp.int32)
        key_doc = lookup_docs(key_pos, doc_of_block)
        visible = (key_doc[None, :] == query_doc[:, None]) & (
            key_pos[None, :] <= query_pos[:, None]
        )
        return update(state_now, query_head_rows, key_piece, value_piece, visible)

    arrivals, shared, own = ring_transfer(out_weight)
    initial_state = fresh_state(kv_heads, group_width, tok_rows)
    state_now = attend(initial_state, keys, values, query_start)
    for distance in range(1, reach_devs + 1):
        prior = passed_along(jnp.concatenate([keys, values], axis=1), "ctx", distance)
        prior_keys, prior_values = prior[:, : keys.shape[1]], prior[:, keys.shape[1] :]
        state_now = attend(state_now, prior_keys, prior_values, query_start - distance * tok_rows)
    attended = finish(state_now, tok_rows, q_heads)
    features = head_features(attended)
    mixed = ring_project(features, arrivals, shared, own, out_weight.shape[0])
    return mixed.astype(jnp.bfloat16)


def solution(mesh):
    return jax.shard_map(
        per_device,
        mesh=mesh,
        in_specs=(
            P(("group", "ctx"), "head"),
            P(("group", "ctx"), "head"),
            P(("group", "ctx"), "head"),
            P("group"),
            P("ctx", "head"),
        ),
        out_specs=P(("group", "ctx"), "head"),
        check_vma=False,
    )
```

```python
import math

import jax
import jax.numpy as jnp
from jax import lax
from jax.sharding import PartitionSpec as P

HEAD_SIZE = 128
BLOCK_TOKENS = 128


def passed_along(array, axis, by):
    peers = lax.axis_size(axis)
    pairs = [(i, i + by) for i in range(peers) if 0 <= i + by < peers]
    return lax.ppermute(array, axis, pairs)


def lookup_docs(positions, doc_of_block):
    block_ids = jnp.floor_divide(positions, BLOCK_TOKENS)
    table_ids = jnp.arange(doc_of_block.shape[0], dtype=jnp.int32)
    matches = block_ids[:, None] == table_ids[None, :]
    return jnp.max(jnp.where(matches, doc_of_block[None, :], -1), axis=1)


def update(state_now, query_head_rows, key_piece, value_piece, visible):
    running_max, summed, totals = state_now
    rows_here = key_piece.shape[0]
    kv_heads = query_head_rows.shape[1]
    key_head_rows = key_piece.reshape(rows_here, kv_heads, HEAD_SIZE)
    value_head_rows = value_piece.reshape(rows_here, kv_heads, HEAD_SIZE)
    score_scale = 1.0 / math.sqrt(HEAD_SIZE)
    scores = (
        jnp.einsum(
            "qhgd,khd->hgqk", query_head_rows, key_head_rows, preferred_element_type=jnp.float32
        )
        * score_scale
    )
    scores = jnp.where(visible, scores, -1e30)
    new_max = jnp.maximum(running_max, jnp.max(scores, axis=-1))
    weights = jnp.where(visible, jnp.exp(scores - new_max[..., None]), 0.0)
    rescale = jnp.exp(running_max - new_max)
    products = jnp.einsum(
        "hgqk,khd->hgqd",
        weights.astype(jnp.bfloat16),
        value_head_rows,
        preferred_element_type=jnp.float32,
    )
    summed = summed * rescale[..., None] + products
    totals = totals * rescale + jnp.sum(weights, axis=-1)
    return (new_max, summed, totals)


def fresh_state(kv_heads, group_width, rows_here):
    return (
        jnp.full((kv_heads, group_width, rows_here), -1e30, jnp.float32),
        jnp.zeros((kv_heads, group_width, rows_here, HEAD_SIZE), jnp.float32),
        jnp.zeros((kv_heads, group_width, rows_here), jnp.float32),
    )


def finish(state_now, rows_here, q_heads):
    running_max, summed, totals = state_now
    attended = summed / totals[..., None]
    return (
        jnp.transpose(attended, (2, 0, 1, 3))
        .reshape(rows_here, q_heads * HEAD_SIZE)
        .astype(jnp.bfloat16)
    )


def head_features(attended):
    head_count = lax.axis_size("head")
    head_index = lax.axis_index("head")
    received = [attended]
    for shift in range(1, head_count):
        pairs = [(i, (i + shift) % head_count) for i in range(head_count)]
        received.append(lax.ppermute(attended, "head", pairs))
    pieces = []
    for source in range(head_count):
        shift_of = (head_index + head_count - source) % head_count
        piece = received[0]
        for shift in range(1, head_count):
            piece = jnp.where(shift_of == shift, received[shift], piece)
        pieces.append(piece)
    return jnp.concatenate(pieces, axis=1)


def ring_transfer(out_weight):
    count = lax.axis_size("ctx")
    order = list(range(0, count, 2)) + sorted(range(1, count, 2), reverse=True)
    position_of = [0] * count
    for position, index in enumerate(order):
        position_of[index] = position
    ctx_index = lax.axis_index("ctx")
    position = jnp.asarray(position_of, jnp.int32)[ctx_index]
    order_table = jnp.asarray(order, jnp.int32)
    columns = out_weight.shape[1]
    groups = lax.axis_size("group")
    group_index = lax.axis_index("group")
    own = (columns // 3) // 128 * 128 if groups == 2 else 0
    shared = columns - groups * own if own else columns
    swap = [(0, 1), (1, 0)]

    def carried(block):
        if not own:
            return block
        mine = lax.dynamic_slice_in_dim(block, shared + group_index * own, own, 1)
        return jnp.concatenate([block[:, :shared], mine], axis=1)

    def other_of(block):
        return lax.dynamic_slice_in_dim(block, shared + (1 - group_index) * own, own, 1)

    arrivals = [(ctx_index, carried(out_weight), other_of(out_weight) if own else None)]
    ahead = [(order[p], order[(p + 1) % count]) for p in range(count)]
    behind = [(order[p], order[(p - 1) % count]) for p in range(count)]
    forward = backward = carried(out_weight)
    forward_steps = count // 2
    backward_steps = count - 1 - forward_steps
    for step in range(1, forward_steps + 1):
        forward = lax.ppermute(forward, "ctx", ahead)
        crossed = lax.ppermute(forward[:, shared:], "group", swap) if own else None
        arrivals.append((order_table[(position + count - step) % count], forward, crossed))
        if step <= backward_steps:
            backward = lax.ppermute(backward, "ctx", behind)
            crossed = lax.ppermute(backward[:, shared:], "group", swap) if own else None
            arrivals.append((order_table[(position + step) % count], backward, crossed))
    return arrivals, shared, own


def ring_project(features, arrivals, shared, own, rows):
    group_index = lax.axis_index("group")
    parts = None
    for source, carried_block, crossed in arrivals:
        piece = lax.dynamic_slice_in_dim(features, source * rows, rows, 1)
        terms = [jnp.dot(piece, carried_block, preferred_element_type=jnp.float32)]
        if own:
            terms.append(jnp.dot(piece, crossed, preferred_element_type=jnp.float32))
        parts = terms if parts is None else [a + b for a, b in zip(parts, terms)]
    if not own:
        return parts[0]
    mine, other = parts[0][:, shared:], parts[1]
    first = jnp.where(group_index == 0, mine, other)
    second = jnp.where(group_index == 0, other, mine)
    return jnp.concatenate([parts[0][:, :shared], first, second], axis=1)

def scatter_project(features, weight_columns):
    count = lax.axis_size("ctx")
    rows = weight_columns.shape[0]
    tokens = features.shape[0]
    chunks = features.reshape(tokens, count, rows)
    mine = lax.all_to_all(chunks, "ctx", 1, 0, tiled=True).reshape(count * tokens, rows)
    partial = jnp.dot(mine, weight_columns, preferred_element_type=jnp.float32)
    return lax.psum_scatter(
        partial.astype(jnp.bfloat16), "ctx", scatter_dimension=0, tiled=True
    )


def per_device(queries, keys, values, doc_of_block, out_weight):
    tok_rows = queries.shape[0]
    kv_heads = keys.shape[1] // HEAD_SIZE
    q_heads = queries.shape[1] // HEAD_SIZE
    group_width = q_heads // kv_heads
    ctx_count = lax.axis_size("ctx")
    reach_devs = min(8, ctx_count // 2)
    ctx_index = lax.axis_index("ctx")
    query_start = ctx_index * tok_rows
    query_pos = query_start + jnp.arange(tok_rows, dtype=jnp.int32)
    query_doc = lookup_docs(query_pos, doc_of_block)
    query_head_rows = queries.reshape(tok_rows, kv_heads, group_width, HEAD_SIZE)

    def attend(state_now, key_piece, value_piece, key_start):
        key_pos = key_start + jnp.arange(key_piece.shape[0], dtype=jnp.int32)
        key_doc = lookup_docs(key_pos, doc_of_block)
        visible = (key_doc[None, :] == query_doc[:, None]) & (
            key_pos[None, :] <= query_pos[:, None]
        )
        return update(state_now, query_head_rows, key_piece, value_piece, visible)

    columns = out_weight.shape[1]
    reduced = (columns // 4) // 128 * 128
    arrivals, shared, own = ring_transfer(out_weight[:, : columns - reduced])
    initial_state = fresh_state(kv_heads, group_width, tok_rows)
    state_now = attend(initial_state, keys, values, query_start)
    for distance in range(1, reach_devs + 1):
        prior_keys, prior_values = passed_along((keys, values), "ctx", distance)
        state_now = attend(state_now, prior_keys, prior_values, query_start - distance * tok_rows)
    attended = finish(state_now, tok_rows, q_heads)
    features = head_features(attended)
    mixed = ring_project(features, arrivals, shared, own, out_weight.shape[0])
    late = [index for index in (3, 4) if index < len(arrivals)]
    tied = lax.optimization_barrier((features, [arrivals[index][1] for index in late]))
    for index, value in zip(late, tied[1]):
        arrivals[index] = (arrivals[index][0], value, arrivals[index][2])
    summed = scatter_project(tied[0], out_weight[:, columns - reduced :])
    return jnp.concatenate([mixed.astype(jnp.bfloat16), summed], axis=1)


def solution(mesh):
    return jax.shard_map(
        per_device,
        mesh=mesh,
        in_specs=(
            P(("group", "ctx"), "head"),
            P(("group", "ctx"), "head"),
            P(("group", "ctx"), "head"),
            P("group"),
            P("ctx", "head"),
        ),
        out_specs=P(("group", "ctx"), "head"),
        check_vma=False,
    )
```

```python
import math

import jax
import jax.numpy as jnp
from jax import lax
from jax.sharding import PartitionSpec as P

HEAD_SIZE = 128
BLOCK_TOKENS = 128


def passed_along(array, axis, by):
    peers = lax.axis_size(axis)
    pairs = [(i, i + by) for i in range(peers) if 0 <= i + by < peers]
    return lax.ppermute(array, axis, pairs)


def lookup_docs(positions, doc_of_block):
    block_ids = jnp.floor_divide(positions, BLOCK_TOKENS)
    table_ids = jnp.arange(doc_of_block.shape[0], dtype=jnp.int32)
    matches = block_ids[:, None] == table_ids[None, :]
    return jnp.max(jnp.where(matches, doc_of_block[None, :], -1), axis=1)


def update(state_now, query_head_rows, key_piece, value_piece, visible):
    running_max, summed, totals = state_now
    rows_here = key_piece.shape[0]
    kv_heads = query_head_rows.shape[1]
    key_head_rows = key_piece.reshape(rows_here, kv_heads, HEAD_SIZE)
    value_head_rows = value_piece.reshape(rows_here, kv_heads, HEAD_SIZE)
    score_scale = 1.0 / math.sqrt(HEAD_SIZE)
    scores = (
        jnp.einsum(
            "qhgd,khd->hgqk", query_head_rows, key_head_rows, preferred_element_type=jnp.float32
        )
        * score_scale
    )
    scores = jnp.where(visible, scores, -1e30)
    new_max = jnp.maximum(running_max, jnp.max(scores, axis=-1))
    weights = jnp.where(visible, jnp.exp(scores - new_max[..., None]), 0.0)
    rescale = jnp.exp(running_max - new_max)
    products = jnp.einsum(
        "hgqk,khd->hgqd",
        weights.astype(jnp.bfloat16),
        value_head_rows,
        preferred_element_type=jnp.float32,
    )
    summed = summed * rescale[..., None] + products
    totals = totals * rescale + jnp.sum(weights, axis=-1)
    return (new_max, summed, totals)


def fresh_state(kv_heads, group_width, rows_here):
    return (
        jnp.full((kv_heads, group_width, rows_here), -1e30, jnp.float32),
        jnp.zeros((kv_heads, group_width, rows_here, HEAD_SIZE), jnp.float32),
        jnp.zeros((kv_heads, group_width, rows_here), jnp.float32),
    )


def finish(state_now, rows_here, q_heads):
    running_max, summed, totals = state_now
    attended = summed / totals[..., None]
    return (
        jnp.transpose(attended, (2, 0, 1, 3))
        .reshape(rows_here, q_heads * HEAD_SIZE)
        .astype(jnp.bfloat16)
    )


def head_features(attended):
    head_count = lax.axis_size("head")
    head_index = lax.axis_index("head")
    received = [attended]
    for shift in range(1, head_count):
        pairs = [(i, (i + shift) % head_count) for i in range(head_count)]
        received.append(lax.ppermute(attended, "head", pairs))
    pieces = []
    for source in range(head_count):
        shift_of = (head_index + head_count - source) % head_count
        piece = received[0]
        for shift in range(1, head_count):
            piece = jnp.where(shift_of == shift, received[shift], piece)
        pieces.append(piece)
    return jnp.concatenate(pieces, axis=1)


def ring_transfer(out_weight):
    count = lax.axis_size("ctx")
    order = list(range(0, count, 2)) + sorted(range(1, count, 2), reverse=True)
    position_of = [0] * count
    for position, index in enumerate(order):
        position_of[index] = position
    ctx_index = lax.axis_index("ctx")
    position = jnp.asarray(position_of, jnp.int32)[ctx_index]
    order_table = jnp.asarray(order, jnp.int32)
    columns = out_weight.shape[1]
    groups = lax.axis_size("group")
    group_index = lax.axis_index("group")
    own = (columns // 3) // 128 * 128 if groups == 2 else 0
    shared = columns - groups * own if own else columns
    swap = [(0, 1), (1, 0)]

    def carried(block):
        if not own:
            return block
        mine = lax.dynamic_slice_in_dim(block, shared + group_index * own, own, 1)
        return jnp.concatenate([block[:, :shared], mine], axis=1)

    def other_of(block):
        return lax.dynamic_slice_in_dim(block, shared + (1 - group_index) * own, own, 1)

    arrivals = [(ctx_index, carried(out_weight), other_of(out_weight) if own else None)]
    ahead = [(order[p], order[(p + 1) % count]) for p in range(count)]
    behind = [(order[p], order[(p - 1) % count]) for p in range(count)]
    forward = backward = carried(out_weight)
    forward_steps = count // 2
    backward_steps = count - 1 - forward_steps
    for step in range(1, forward_steps + 1):
        if step > backward_steps:
            half = forward.shape[1] // 2
            forward = lax.ppermute(forward[:, :half], "ctx", ahead)
            backward = lax.ppermute(backward[:, half:], "ctx", behind)
            joined = jnp.concatenate([forward, backward], axis=1)
            crossed = lax.ppermute(joined[:, shared:], "group", swap) if own else None
            arrivals.append((order_table[(position + count - step) % count], joined, crossed))
            break
        forward = lax.ppermute(forward, "ctx", ahead)
        crossed = lax.ppermute(forward[:, shared:], "group", swap) if own else None
        arrivals.append((order_table[(position + count - step) % count], forward, crossed))
        if step <= backward_steps:
            backward = lax.ppermute(backward, "ctx", behind)
            crossed = lax.ppermute(backward[:, shared:], "group", swap) if own else None
            arrivals.append((order_table[(position + step) % count], backward, crossed))
    return arrivals, shared, own


def ring_project(features, arrivals, shared, own, rows):
    group_index = lax.axis_index("group")
    parts = None
    for source, carried_block, crossed in arrivals:
        piece = lax.dynamic_slice_in_dim(features, source * rows, rows, 1)
        terms = [jnp.dot(piece, carried_block, preferred_element_type=jnp.float32)]
        if own:
            terms.append(jnp.dot(piece, crossed, preferred_element_type=jnp.float32))
        parts = terms if parts is None else [a + b for a, b in zip(parts, terms)]
    if not own:
        return parts[0]
    mine, other = parts[0][:, shared:], parts[1]
    first = jnp.where(group_index == 0, mine, other)
    second = jnp.where(group_index == 0, other, mine)
    return jnp.concatenate([parts[0][:, :shared], first, second], axis=1)

def per_device(queries, keys, values, doc_of_block, out_weight):
    tok_rows = queries.shape[0]
    kv_heads = keys.shape[1] // HEAD_SIZE
    q_heads = queries.shape[1] // HEAD_SIZE
    group_width = q_heads // kv_heads
    ctx_count = lax.axis_size("ctx")
    reach_devs = min(8, ctx_count // 2)
    ctx_index = lax.axis_index("ctx")
    query_start = ctx_index * tok_rows
    query_pos = query_start + jnp.arange(tok_rows, dtype=jnp.int32)
    query_doc = lookup_docs(query_pos, doc_of_block)
    query_head_rows = queries.reshape(tok_rows, kv_heads, group_width, HEAD_SIZE)

    def attend(state_now, key_piece, value_piece, key_start):
        key_pos = key_start + jnp.arange(key_piece.shape[0], dtype=jnp.int32)
        key_doc = lookup_docs(key_pos, doc_of_block)
        visible = (key_doc[None, :] == query_doc[:, None]) & (
            key_pos[None, :] <= query_pos[:, None]
        )
        return update(state_now, query_head_rows, key_piece, value_piece, visible)

    arrivals, shared, own = ring_transfer(out_weight)
    initial_state = fresh_state(kv_heads, group_width, tok_rows)
    state_now = attend(initial_state, keys, values, query_start)
    for distance in range(1, reach_devs + 1):
        prior_keys, prior_values = passed_along((keys, values), "ctx", distance)
        state_now = attend(state_now, prior_keys, prior_values, query_start - distance * tok_rows)
    attended = finish(state_now, tok_rows, q_heads)
    features = head_features(attended)
    mixed = ring_project(features, arrivals, shared, own, out_weight.shape[0])
    return mixed.astype(jnp.bfloat16)


def solution(mesh):
    return jax.shard_map(
        per_device,
        mesh=mesh,
        in_specs=(
            P(("group", "ctx"), "head"),
            P(("group", "ctx"), "head"),
            P(("group", "ctx"), "head"),
            P("group"),
            P("ctx", "head"),
        ),
        out_specs=P(("group", "ctx"), "head"),
        check_vma=False,
    )
```

```python
import math

import jax
import jax.numpy as jnp
from jax import lax
from jax.sharding import PartitionSpec as P

HEAD_SIZE = 128
BLOCK_TOKENS = 128


def passed_along(array, axis, by):
    peers = lax.axis_size(axis)
    pairs = [(i, i + by) for i in range(peers) if 0 <= i + by < peers]
    return lax.ppermute(array, axis, pairs)


def lookup_docs(positions, doc_of_block):
    block_ids = jnp.floor_divide(positions, BLOCK_TOKENS)
    table_ids = jnp.arange(doc_of_block.shape[0], dtype=jnp.int32)
    matches = block_ids[:, None] == table_ids[None, :]
    return jnp.max(jnp.where(matches, doc_of_block[None, :], -1), axis=1)


def update(state_now, query_head_rows, key_piece, value_piece, visible):
    running_max, summed, totals = state_now
    rows_here = key_piece.shape[0]
    kv_heads = query_head_rows.shape[1]
    key_head_rows = key_piece.reshape(rows_here, kv_heads, HEAD_SIZE)
    value_head_rows = value_piece.reshape(rows_here, kv_heads, HEAD_SIZE)
    score_scale = 1.0 / math.sqrt(HEAD_SIZE)
    scores = (
        jnp.einsum(
            "qhgd,khd->hgqk", query_head_rows, key_head_rows, preferred_element_type=jnp.float32
        )
        * score_scale
    )
    scores = jnp.where(visible, scores, -1e30)
    new_max = jnp.maximum(running_max, jnp.max(scores, axis=-1))
    weights = jnp.where(visible, jnp.exp(scores - new_max[..., None]), 0.0)
    rescale = jnp.exp(running_max - new_max)
    products = jnp.einsum(
        "hgqk,khd->hgqd",
        weights.astype(jnp.bfloat16),
        value_head_rows,
        preferred_element_type=jnp.float32,
    )
    summed = summed * rescale[..., None] + products
    totals = totals * rescale + jnp.sum(weights, axis=-1)
    return (new_max, summed, totals)


def fresh_state(kv_heads, group_width, rows_here):
    return (
        jnp.full((kv_heads, group_width, rows_here), -1e30, jnp.float32),
        jnp.zeros((kv_heads, group_width, rows_here, HEAD_SIZE), jnp.float32),
        jnp.zeros((kv_heads, group_width, rows_here), jnp.float32),
    )


def finish(state_now, rows_here, q_heads):
    running_max, summed, totals = state_now
    attended = summed / totals[..., None]
    return (
        jnp.transpose(attended, (2, 0, 1, 3))
        .reshape(rows_here, q_heads * HEAD_SIZE)
        .astype(jnp.bfloat16)
    )


def head_features(attended):
    head_count = lax.axis_size("head")
    head_index = lax.axis_index("head")
    received = [attended]
    for shift in range(1, head_count):
        pairs = [(i, (i + shift) % head_count) for i in range(head_count)]
        received.append(lax.ppermute(attended, "head", pairs))
    pieces = []
    for source in range(head_count):
        shift_of = (head_index + head_count - source) % head_count
        piece = received[0]
        for shift in range(1, head_count):
            piece = jnp.where(shift_of == shift, received[shift], piece)
        pieces.append(piece)
    return jnp.concatenate(pieces, axis=1)


def ring_transfer(out_weight):
    count = lax.axis_size("ctx")
    order = list(range(0, count, 2)) + sorted(range(1, count, 2), reverse=True)
    position_of = [0] * count
    for position, index in enumerate(order):
        position_of[index] = position
    ctx_index = lax.axis_index("ctx")
    position = jnp.asarray(position_of, jnp.int32)[ctx_index]
    order_table = jnp.asarray(order, jnp.int32)
    columns = out_weight.shape[1]
    groups = lax.axis_size("group")
    group_index = lax.axis_index("group")
    own = (columns // 3) // 128 * 128 if groups == 2 else 0
    shared = columns - groups * own if own else columns
    swap = [(0, 1), (1, 0)]

    def carried(block):
        if not own:
            return block
        mine = lax.dynamic_slice_in_dim(block, shared + group_index * own, own, 1)
        return jnp.concatenate([block[:, :shared], mine], axis=1)

    def other_of(block):
        return lax.dynamic_slice_in_dim(block, shared + (1 - group_index) * own, own, 1)

    arrivals = [(ctx_index, carried(out_weight), other_of(out_weight) if own else None)]
    ahead = [(order[p], order[(p + 1) % count]) for p in range(count)]
    behind = [(order[p], order[(p - 1) % count]) for p in range(count)]
    forward = backward = carried(out_weight)
    forward_steps = count // 2
    backward_steps = count - 1 - forward_steps
    for step in range(1, forward_steps + 1):
        forward = lax.ppermute(forward, "ctx", ahead)
        crossed = lax.ppermute(forward[:, shared:], "group", swap) if own else None
        arrivals.append((order_table[(position + count - step) % count], forward, crossed))
        if step <= backward_steps:
            backward = lax.ppermute(backward, "ctx", behind)
            crossed = lax.ppermute(backward[:, shared:], "group", swap) if own else None
            arrivals.append((order_table[(position + step) % count], backward, crossed))
    return arrivals, shared, own


def ring_project(features, arrivals, shared, own, rows):
    group_index = lax.axis_index("group")
    parts = None
    for source, carried_block, crossed in arrivals:
        piece = lax.dynamic_slice_in_dim(features, source * rows, rows, 1)
        terms = [jnp.dot(piece, carried_block, preferred_element_type=jnp.float32)]
        if own:
            terms.append(jnp.dot(piece, crossed, preferred_element_type=jnp.float32))
        parts = terms if parts is None else [a + b for a, b in zip(parts, terms)]
    if not own:
        return parts[0]
    mine, other = parts[0][:, shared:], parts[1]
    first = jnp.where(group_index == 0, mine, other)
    second = jnp.where(group_index == 0, other, mine)
    return jnp.concatenate([parts[0][:, :shared], first, second], axis=1)

def per_device(queries, keys, values, doc_of_block, out_weight):
    tok_rows = queries.shape[0]
    kv_heads = keys.shape[1] // HEAD_SIZE
    q_heads = queries.shape[1] // HEAD_SIZE
    group_width = q_heads // kv_heads
    ctx_count = lax.axis_size("ctx")
    reach_devs = min(8, ctx_count // 2)
    ctx_index = lax.axis_index("ctx")
    query_start = ctx_index * tok_rows
    query_pos = query_start + jnp.arange(tok_rows, dtype=jnp.int32)
    query_doc = lookup_docs(query_pos, doc_of_block)
    query_head_rows = queries.reshape(tok_rows, kv_heads, group_width, HEAD_SIZE)

    def attend(state_now, key_piece, value_piece, key_start):
        key_pos = key_start + jnp.arange(key_piece.shape[0], dtype=jnp.int32)
        key_doc = lookup_docs(key_pos, doc_of_block)
        visible = (key_doc[None, :] == query_doc[:, None]) & (
            key_pos[None, :] <= query_pos[:, None]
        )
        return update(state_now, query_head_rows, key_piece, value_piece, visible)

    arrivals, shared, own = ring_transfer(out_weight)
    initial_state = fresh_state(kv_heads, group_width, tok_rows)
    state_now = attend(initial_state, keys, values, query_start)
    for distance in range(1, reach_devs + 1):
        skipped = BLOCK_TOKENS if distance == reach_devs and tok_rows > BLOCK_TOKENS else 0
        prior_keys, prior_values = passed_along((keys[skipped:], values[skipped:]), "ctx", distance)
        key_start = query_start - distance * tok_rows + skipped
        state_now = attend(state_now, prior_keys, prior_values, key_start)
    attended = finish(state_now, tok_rows, q_heads)
    features = head_features(attended)
    mixed = ring_project(features, arrivals, shared, own, out_weight.shape[0])
    return mixed.astype(jnp.bfloat16)


def solution(mesh):
    return jax.shard_map(
        per_device,
        mesh=mesh,
        in_specs=(
            P(("group", "ctx"), "head"),
            P(("group", "ctx"), "head"),
            P(("group", "ctx"), "head"),
            P("group"),
            P("ctx", "head"),
        ),
        out_specs=P(("group", "ctx"), "head"),
        check_vma=False,
    )
```

```python
import math

import jax
import jax.numpy as jnp
from jax import lax
from jax.sharding import PartitionSpec as P

HEAD_SIZE = 128
BLOCK_TOKENS = 128


def passed_along(array, axis, by):
    peers = lax.axis_size(axis)
    pairs = [(i, i + by) for i in range(peers) if 0 <= i + by < peers]
    return lax.ppermute(array, axis, pairs)


def lookup_docs(positions, doc_of_block):
    block_ids = jnp.floor_divide(positions, BLOCK_TOKENS)
    table_ids = jnp.arange(doc_of_block.shape[0], dtype=jnp.int32)
    matches = block_ids[:, None] == table_ids[None, :]
    return jnp.max(jnp.where(matches, doc_of_block[None, :], -1), axis=1)


def update(state_now, query_head_rows, key_piece, value_piece, visible):
    running_max, summed, totals = state_now
    rows_here = key_piece.shape[0]
    kv_heads = query_head_rows.shape[1]
    key_head_rows = key_piece.reshape(rows_here, kv_heads, HEAD_SIZE)
    value_head_rows = value_piece.reshape(rows_here, kv_heads, HEAD_SIZE)
    score_scale = 1.0 / math.sqrt(HEAD_SIZE)
    scores = (
        jnp.einsum(
            "qhgd,khd->hgqk", query_head_rows, key_head_rows, preferred_element_type=jnp.float32
        )
        * score_scale
    )
    scores = jnp.where(visible, scores, -1e30)
    new_max = jnp.maximum(running_max, jnp.max(scores, axis=-1))
    weights = jnp.where(visible, jnp.exp(scores - new_max[..., None]), 0.0)
    rescale = jnp.exp(running_max - new_max)
    products = jnp.einsum(
        "hgqk,khd->hgqd",
        weights.astype(jnp.bfloat16),
        value_head_rows,
        preferred_element_type=jnp.float32,
    )
    summed = summed * rescale[..., None] + products
    totals = totals * rescale + jnp.sum(weights, axis=-1)
    return (new_max, summed, totals)


def fresh_state(kv_heads, group_width, rows_here):
    return (
        jnp.full((kv_heads, group_width, rows_here), -1e30, jnp.float32),
        jnp.zeros((kv_heads, group_width, rows_here, HEAD_SIZE), jnp.float32),
        jnp.zeros((kv_heads, group_width, rows_here), jnp.float32),
    )


def finish(state_now, rows_here, q_heads):
    running_max, summed, totals = state_now
    attended = summed / totals[..., None]
    return (
        jnp.transpose(attended, (2, 0, 1, 3))
        .reshape(rows_here, q_heads * HEAD_SIZE)
        .astype(jnp.bfloat16)
    )


def head_features(attended):
    head_count = lax.axis_size("head")
    head_index = lax.axis_index("head")
    received = [attended]
    for shift in range(1, head_count):
        pairs = [(i, (i + shift) % head_count) for i in range(head_count)]
        received.append(lax.ppermute(attended, "head", pairs))
    pieces = []
    for source in range(head_count):
        shift_of = (head_index + head_count - source) % head_count
        piece = received[0]
        for shift in range(1, head_count):
            piece = jnp.where(shift_of == shift, received[shift], piece)
        pieces.append(piece)
    return jnp.concatenate(pieces, axis=1)


def ring_transfer(out_weight):
    count = lax.axis_size("ctx")
    order = list(range(0, count, 2)) + sorted(range(1, count, 2), reverse=True)
    position_of = [0] * count
    for position, index in enumerate(order):
        position_of[index] = position
    ctx_index = lax.axis_index("ctx")
    position = jnp.asarray(position_of, jnp.int32)[ctx_index]
    order_table = jnp.asarray(order, jnp.int32)
    columns = out_weight.shape[1]
    groups = lax.axis_size("group")
    group_index = lax.axis_index("group")
    own = (columns // 4) // 128 * 128 if groups == 2 else 0
    shared = columns - groups * own if own else columns
    swap = [(0, 1), (1, 0)]

    def carried(block):
        if not own:
            return block
        mine = lax.dynamic_slice_in_dim(block, shared + group_index * own, own, 1)
        return jnp.concatenate([block[:, :shared], mine], axis=1)

    def other_of(block):
        return lax.dynamic_slice_in_dim(block, shared + (1 - group_index) * own, own, 1)

    arrivals = [(ctx_index, carried(out_weight), other_of(out_weight) if own else None)]
    ahead = [(order[p], order[(p + 1) % count]) for p in range(count)]
    behind = [(order[p], order[(p - 1) % count]) for p in range(count)]
    forward = backward = carried(out_weight)
    forward_steps = count // 2
    backward_steps = count - 1 - forward_steps
    for step in range(1, forward_steps + 1):
        forward = lax.ppermute(forward, "ctx", ahead)
        crossed = lax.ppermute(forward[:, shared:], "group", swap) if own else None
        arrivals.append((order_table[(position + count - step) % count], forward, crossed))
        if step <= backward_steps:
            backward = lax.ppermute(backward, "ctx", behind)
            crossed = lax.ppermute(backward[:, shared:], "group", swap) if own else None
            arrivals.append((order_table[(position + step) % count], backward, crossed))
    return arrivals, shared, own


def ring_project(features, arrivals, shared, own, rows):
    group_index = lax.axis_index("group")
    parts = None
    for source, carried_block, crossed in arrivals:
        piece = lax.dynamic_slice_in_dim(features, source * rows, rows, 1)
        terms = [jnp.dot(piece, carried_block, preferred_element_type=jnp.float32)]
        if own:
            terms.append(jnp.dot(piece, crossed, preferred_element_type=jnp.float32))
        parts = terms if parts is None else [a + b for a, b in zip(parts, terms)]
    if not own:
        return parts[0]
    mine, other = parts[0][:, shared:], parts[1]
    first = jnp.where(group_index == 0, mine, other)
    second = jnp.where(group_index == 0, other, mine)
    return jnp.concatenate([parts[0][:, :shared], first, second], axis=1)

def per_device(queries, keys, values, doc_of_block, out_weight):
    tok_rows = queries.shape[0]
    kv_heads = keys.shape[1] // HEAD_SIZE
    q_heads = queries.shape[1] // HEAD_SIZE
    group_width = q_heads // kv_heads
    ctx_count = lax.axis_size("ctx")
    reach_devs = min(8, ctx_count // 2)
    ctx_index = lax.axis_index("ctx")
    query_start = ctx_index * tok_rows
    query_pos = query_start + jnp.arange(tok_rows, dtype=jnp.int32)
    query_doc = lookup_docs(query_pos, doc_of_block)
    query_head_rows = queries.reshape(tok_rows, kv_heads, group_width, HEAD_SIZE)

    def attend(state_now, key_piece, value_piece, key_start):
        key_pos = key_start + jnp.arange(key_piece.shape[0], dtype=jnp.int32)
        key_doc = lookup_docs(key_pos, doc_of_block)
        visible = (key_doc[None, :] == query_doc[:, None]) & (
            key_pos[None, :] <= query_pos[:, None]
        )
        return update(state_now, query_head_rows, key_piece, value_piece, visible)

    arrivals, shared, own = ring_transfer(out_weight)
    initial_state = fresh_state(kv_heads, group_width, tok_rows)
    state_now = attend(initial_state, keys, values, query_start)
    for distance in range(1, reach_devs + 1):
        prior_keys, prior_values = passed_along((keys, values), "ctx", distance)
        state_now = attend(state_now, prior_keys, prior_values, query_start - distance * tok_rows)
    attended = finish(state_now, tok_rows, q_heads)
    features = head_features(attended)
    mixed = ring_project(features, arrivals, shared, own, out_weight.shape[0])
    return mixed.astype(jnp.bfloat16)


def solution(mesh):
    return jax.shard_map(
        per_device,
        mesh=mesh,
        in_specs=(
            P(("group", "ctx"), "head"),
            P(("group", "ctx"), "head"),
            P(("group", "ctx"), "head"),
            P("group"),
            P("ctx", "head"),
        ),
        out_specs=P(("group", "ctx"), "head"),
        check_vma=False,
    )
```

```python
import math

import jax
import jax.numpy as jnp
from jax import lax
from jax.sharding import PartitionSpec as P

HEAD_SIZE = 128
BLOCK_TOKENS = 128


def passed_along(array, axis, by):
    peers = lax.axis_size(axis)
    pairs = [(i, i + by) for i in range(peers) if 0 <= i + by < peers]
    return lax.ppermute(array, axis, pairs)


def lookup_docs(positions, doc_of_block):
    block_ids = jnp.floor_divide(positions, BLOCK_TOKENS)
    table_ids = jnp.arange(doc_of_block.shape[0], dtype=jnp.int32)
    matches = block_ids[:, None] == table_ids[None, :]
    return jnp.max(jnp.where(matches, doc_of_block[None, :], -1), axis=1)


def update(state_now, query_head_rows, key_piece, value_piece, visible):
    running_max, summed, totals = state_now
    rows_here = key_piece.shape[0]
    kv_heads = query_head_rows.shape[1]
    key_head_rows = key_piece.reshape(rows_here, kv_heads, HEAD_SIZE)
    value_head_rows = value_piece.reshape(rows_here, kv_heads, HEAD_SIZE)
    score_scale = 1.0 / math.sqrt(HEAD_SIZE)
    scores = (
        jnp.einsum(
            "qhgd,khd->hgqk", query_head_rows, key_head_rows, preferred_element_type=jnp.float32
        )
        * score_scale
    )
    scores = jnp.where(visible, scores, -1e30)
    new_max = jnp.maximum(running_max, jnp.max(scores, axis=-1))
    weights = jnp.where(visible, jnp.exp(scores - new_max[..., None]), 0.0)
    rescale = jnp.exp(running_max - new_max)
    products = jnp.einsum(
        "hgqk,khd->hgqd",
        weights.astype(jnp.bfloat16),
        value_head_rows,
        preferred_element_type=jnp.float32,
    )
    summed = summed * rescale[..., None] + products
    totals = totals * rescale + jnp.sum(weights, axis=-1)
    return (new_max, summed, totals)


def fresh_state(kv_heads, group_width, rows_here):
    return (
        jnp.full((kv_heads, group_width, rows_here), -1e30, jnp.float32),
        jnp.zeros((kv_heads, group_width, rows_here, HEAD_SIZE), jnp.float32),
        jnp.zeros((kv_heads, group_width, rows_here), jnp.float32),
    )


def finish(state_now, rows_here, q_heads):
    running_max, summed, totals = state_now
    attended = summed / totals[..., None]
    return (
        jnp.transpose(attended, (2, 0, 1, 3))
        .reshape(rows_here, q_heads * HEAD_SIZE)
        .astype(jnp.bfloat16)
    )


def head_features(attended):
    head_count = lax.axis_size("head")
    head_index = lax.axis_index("head")
    received = [attended]
    for shift in range(1, head_count):
        pairs = [(i, (i + shift) % head_count) for i in range(head_count)]
        received.append(lax.ppermute(attended, "head", pairs))
    pieces = []
    for source in range(head_count):
        shift_of = (head_index + head_count - source) % head_count
        piece = received[0]
        for shift in range(1, head_count):
            piece = jnp.where(shift_of == shift, received[shift], piece)
        pieces.append(piece)
    return jnp.concatenate(pieces, axis=1)


class Split:
    def __init__(self, columns, own):
        self.own = own
        self.shared = columns - 2 * own if own else columns

    def carried(self, block, group_index):
        if not self.own:
            return block
        start = self.shared + group_index * self.own
        mine = lax.dynamic_slice_in_dim(block, start, self.own, 1)
        return jnp.concatenate([block[:, : self.shared], mine], axis=1)

    def other_of(self, block, group_index):
        start = self.shared + (1 - group_index) * self.own
        return lax.dynamic_slice_in_dim(block, start, self.own, 1)


def ring_transfer(out_weight):
    count = lax.axis_size("ctx")
    order = list(range(0, count, 2)) + sorted(range(1, count, 2), reverse=True)
    position_of = [0] * count
    for position, index in enumerate(order):
        position_of[index] = position
    ctx_index = lax.axis_index("ctx")
    position = jnp.asarray(position_of, jnp.int32)[ctx_index]
    order_table = jnp.asarray(order, jnp.int32)
    columns = out_weight.shape[1]
    groups = lax.axis_size("group")
    group_index = lax.axis_index("group")
    lanes = columns // 128
    ahead_split = Split(columns, (lanes * 5 // 16) * 128 if groups == 2 else 0)
    behind_split = Split(columns, (lanes * 3 // 16) * 128 if groups == 2 else 0)
    swap = [(0, 1), (1, 0)]

    def cross(block, split):
        if not split.own:
            return None
        return lax.ppermute(block[:, split.shared :], "group", swap)

    own_other = ahead_split.other_of(out_weight, group_index) if ahead_split.own else None
    arrivals = [(ctx_index, ahead_split.carried(out_weight, group_index), own_other, ahead_split)]
    ahead = [(order[p], order[(p + 1) % count]) for p in range(count)]
    behind = [(order[p], order[(p - 1) % count]) for p in range(count)]
    forward = ahead_split.carried(out_weight, group_index)
    backward = behind_split.carried(out_weight, group_index)
    forward_steps = count // 2
    backward_steps = count - 1 - forward_steps
    for step in range(1, forward_steps + 1):
        forward = lax.ppermute(forward, "ctx", ahead)
        arrivals.append(
            (order_table[(position + count - step) % count], forward, cross(forward, ahead_split), ahead_split)
        )
        if step <= backward_steps:
            backward = lax.ppermute(backward, "ctx", behind)
            arrivals.append(
                (order_table[(position + step) % count], backward, cross(backward, behind_split), behind_split)
            )
    return arrivals


def ring_project(features, arrivals, rows):
    group_index = lax.axis_index("group")
    sums = {}
    for source, carried_block, crossed, split in arrivals:
        piece = lax.dynamic_slice_in_dim(features, source * rows, rows, 1)
        terms = [jnp.dot(piece, carried_block, preferred_element_type=jnp.float32)]
        if split.own:
            terms.append(jnp.dot(piece, crossed, preferred_element_type=jnp.float32))
        key = id(split)
        if key in sums:
            sums[key] = (split, [a + b for a, b in zip(sums[key][1], terms)])
        else:
            sums[key] = (split, terms)
    mixed = None
    for split, parts in sums.values():
        if split.own:
            mine, other = parts[0][:, split.shared :], parts[1]
            first = jnp.where(group_index == 0, mine, other)
            second = jnp.where(group_index == 0, other, mine)
            full = jnp.concatenate([parts[0][:, : split.shared], first, second], axis=1)
        else:
            full = parts[0]
        mixed = full if mixed is None else mixed + full
    return mixed


def per_device(queries, keys, values, doc_of_block, out_weight):
    tok_rows = queries.shape[0]
    kv_heads = keys.shape[1] // HEAD_SIZE
    q_heads = queries.shape[1] // HEAD_SIZE
    group_width = q_heads // kv_heads
    ctx_count = lax.axis_size("ctx")
    reach_devs = min(8, ctx_count // 2)
    ctx_index = lax.axis_index("ctx")
    query_start = ctx_index * tok_rows
    query_pos = query_start + jnp.arange(tok_rows, dtype=jnp.int32)
    query_doc = lookup_docs(query_pos, doc_of_block)
    query_head_rows = queries.reshape(tok_rows, kv_heads, group_width, HEAD_SIZE)

    def attend(state_now, key_piece, value_piece, key_start):
        key_pos = key_start + jnp.arange(key_piece.shape[0], dtype=jnp.int32)
        key_doc = lookup_docs(key_pos, doc_of_block)
        visible = (key_doc[None, :] == query_doc[:, None]) & (
            key_pos[None, :] <= query_pos[:, None]
        )
        return update(state_now, query_head_rows, key_piece, value_piece, visible)

    arrivals = ring_transfer(out_weight)
    initial_state = fresh_state(kv_heads, group_width, tok_rows)
    state_now = attend(initial_state, keys, values, query_start)
    for distance in range(1, reach_devs + 1):
        prior_keys, prior_values = passed_along((keys, values), "ctx", distance)
        state_now = attend(state_now, prior_keys, prior_values, query_start - distance * tok_rows)
    attended = finish(state_now, tok_rows, q_heads)
    features = head_features(attended)
    mixed = ring_project(features, arrivals, out_weight.shape[0])
    return mixed.astype(jnp.bfloat16)


def solution(mesh):
    return jax.shard_map(
        per_device,
        mesh=mesh,
        in_specs=(
            P(("group", "ctx"), "head"),
            P(("group", "ctx"), "head"),
            P(("group", "ctx"), "head"),
            P("group"),
            P("ctx", "head"),
        ),
        out_specs=P(("group", "ctx"), "head"),
        check_vma=False,
    )
```

```python
import math

import jax
import jax.numpy as jnp
from jax import lax
from jax.sharding import PartitionSpec as P

HEAD_SIZE = 128
BLOCK_TOKENS = 128


def passed_along(array, axis, by):
    peers = lax.axis_size(axis)
    pairs = [(i, i + by) for i in range(peers) if 0 <= i + by < peers]
    return lax.ppermute(array, axis, pairs)


def lookup_docs(positions, doc_of_block):
    block_ids = jnp.floor_divide(positions, BLOCK_TOKENS)
    table_ids = jnp.arange(doc_of_block.shape[0], dtype=jnp.int32)
    matches = block_ids[:, None] == table_ids[None, :]
    return jnp.max(jnp.where(matches, doc_of_block[None, :], -1), axis=1)


def update(state_now, query_head_rows, key_piece, value_piece, visible):
    running_max, summed, totals = state_now
    rows_here = key_piece.shape[0]
    kv_heads = query_head_rows.shape[1]
    key_head_rows = key_piece.reshape(rows_here, kv_heads, HEAD_SIZE)
    value_head_rows = value_piece.reshape(rows_here, kv_heads, HEAD_SIZE)
    score_scale = 1.0 / math.sqrt(HEAD_SIZE)
    scores = (
        jnp.einsum(
            "qhgd,khd->hgqk", query_head_rows, key_head_rows, preferred_element_type=jnp.float32
        )
        * score_scale
    )
    scores = jnp.where(visible, scores, -1e30)
    new_max = jnp.maximum(running_max, jnp.max(scores, axis=-1))
    weights = jnp.where(visible, jnp.exp(scores - new_max[..., None]), 0.0)
    rescale = jnp.exp(running_max - new_max)
    products = jnp.einsum(
        "hgqk,khd->hgqd",
        weights.astype(jnp.bfloat16),
        value_head_rows,
        preferred_element_type=jnp.float32,
    )
    summed = summed * rescale[..., None] + products
    totals = totals * rescale + jnp.sum(weights, axis=-1)
    return (new_max, summed, totals)


def fresh_state(kv_heads, group_width, rows_here):
    return (
        jnp.full((kv_heads, group_width, rows_here), -1e30, jnp.float32),
        jnp.zeros((kv_heads, group_width, rows_here, HEAD_SIZE), jnp.float32),
        jnp.zeros((kv_heads, group_width, rows_here), jnp.float32),
    )


def finish(state_now, rows_here, q_heads):
    running_max, summed, totals = state_now
    attended = summed / totals[..., None]
    return (
        jnp.transpose(attended, (2, 0, 1, 3))
        .reshape(rows_here, q_heads * HEAD_SIZE)
        .astype(jnp.bfloat16)
    )


def head_features(attended):
    head_count = lax.axis_size("head")
    head_index = lax.axis_index("head")
    received = [attended]
    for shift in range(1, head_count):
        pairs = [(i, (i + shift) % head_count) for i in range(head_count)]
        received.append(lax.ppermute(attended, "head", pairs))
    pieces = []
    for source in range(head_count):
        shift_of = (head_index + head_count - source) % head_count
        piece = received[0]
        for shift in range(1, head_count):
            piece = jnp.where(shift_of == shift, received[shift], piece)
        pieces.append(piece)
    return jnp.concatenate(pieces, axis=1)


def ring_transfer(out_weight):
    count = lax.axis_size("ctx")
    order = list(range(0, count, 2)) + sorted(range(1, count, 2), reverse=True)
    position_of = [0] * count
    for position, index in enumerate(order):
        position_of[index] = position
    ctx_index = lax.axis_index("ctx")
    position = jnp.asarray(position_of, jnp.int32)[ctx_index]
    order_table = jnp.asarray(order, jnp.int32)
    columns = out_weight.shape[1]
    groups = lax.axis_size("group")
    group_index = lax.axis_index("group")
    own = (columns // 16 * 3) // 128 * 128 if groups == 2 else 0
    shared = columns - groups * own if own else columns
    swap = [(0, 1), (1, 0)]

    def carried(block):
        if not own:
            return block
        mine = lax.dynamic_slice_in_dim(block, shared + group_index * own, own, 1)
        return jnp.concatenate([block[:, :shared], mine], axis=1)

    def other_of(block):
        return lax.dynamic_slice_in_dim(block, shared + (1 - group_index) * own, own, 1)

    arrivals = [(ctx_index, carried(out_weight), other_of(out_weight) if own else None)]
    ahead = [(order[p], order[(p + 1) % count]) for p in range(count)]
    behind = [(order[p], order[(p - 1) % count]) for p in range(count)]
    forward = backward = carried(out_weight)
    forward_steps = count // 2
    backward_steps = count - 1 - forward_steps
    for step in range(1, forward_steps + 1):
        forward = lax.ppermute(forward, "ctx", ahead)
        crossed = lax.ppermute(forward[:, shared:], "group", swap) if own else None
        arrivals.append((order_table[(position + count - step) % count], forward, crossed))
        if step <= backward_steps:
            backward = lax.ppermute(backward, "ctx", behind)
            crossed = lax.ppermute(backward[:, shared:], "group", swap) if own else None
            arrivals.append((order_table[(position + step) % count], backward, crossed))
    return arrivals, shared, own


def ring_project(features, arrivals, shared, own, rows):
    group_index = lax.axis_index("group")
    parts = None
    for source, carried_block, crossed in arrivals:
        piece = lax.dynamic_slice_in_dim(features, source * rows, rows, 1)
        terms = [jnp.dot(piece, carried_block, preferred_element_type=jnp.float32)]
        if own:
            terms.append(jnp.dot(piece, crossed, preferred_element_type=jnp.float32))
        parts = terms if parts is None else [a + b for a, b in zip(parts, terms)]
    if not own:
        return parts[0]
    mine, other = parts[0][:, shared:], parts[1]
    first = jnp.where(group_index == 0, mine, other)
    second = jnp.where(group_index == 0, other, mine)
    return jnp.concatenate([parts[0][:, :shared], first, second], axis=1)

def per_device(queries, keys, values, doc_of_block, out_weight):
    tok_rows = queries.shape[0]
    kv_heads = keys.shape[1] // HEAD_SIZE
    q_heads = queries.shape[1] // HEAD_SIZE
    group_width = q_heads // kv_heads
    ctx_count = lax.axis_size("ctx")
    reach_devs = min(8, ctx_count // 2)
    ctx_index = lax.axis_index("ctx")
    query_start = ctx_index * tok_rows
    query_pos = query_start + jnp.arange(tok_rows, dtype=jnp.int32)
    query_doc = lookup_docs(query_pos, doc_of_block)
    query_head_rows = queries.reshape(tok_rows, kv_heads, group_width, HEAD_SIZE)

    def attend(state_now, key_piece, value_piece, key_start):
        key_pos = key_start + jnp.arange(key_piece.shape[0], dtype=jnp.int32)
        key_doc = lookup_docs(key_pos, doc_of_block)
        visible = (key_doc[None, :] == query_doc[:, None]) & (
            key_pos[None, :] <= query_pos[:, None]
        )
        return update(state_now, query_head_rows, key_piece, value_piece, visible)

    arrivals, shared, own = ring_transfer(out_weight)
    initial_state = fresh_state(kv_heads, group_width, tok_rows)
    state_now = attend(initial_state, keys, values, query_start)
    for distance in range(1, reach_devs + 1):
        prior_keys, prior_values = passed_along((keys, values), "ctx", distance)
        state_now = attend(state_now, prior_keys, prior_values, query_start - distance * tok_rows)
    attended = finish(state_now, tok_rows, q_heads)
    features = head_features(attended)
    mixed = ring_project(features, arrivals, shared, own, out_weight.shape[0])
    return mixed.astype(jnp.bfloat16)


def solution(mesh):
    return jax.shard_map(
        per_device,
        mesh=mesh,
        in_specs=(
            P(("group", "ctx"), "head"),
            P(("group", "ctx"), "head"),
            P(("group", "ctx"), "head"),
            P("group"),
            P("ctx", "head"),
        ),
        out_specs=P(("group", "ctx"), "head"),
        check_vma=False,
    )
```

```python
import math

import jax
import jax.numpy as jnp
from jax import lax
from jax.sharding import PartitionSpec as P

HEAD_SIZE = 128
BLOCK_TOKENS = 128


def passed_along(array, axis, by):
    peers = lax.axis_size(axis)
    pairs = [(i, i + by) for i in range(peers) if 0 <= i + by < peers]
    return lax.ppermute(array, axis, pairs)


def lookup_docs(positions, doc_of_block):
    block_ids = jnp.floor_divide(positions, BLOCK_TOKENS)
    table_ids = jnp.arange(doc_of_block.shape[0], dtype=jnp.int32)
    matches = block_ids[:, None] == table_ids[None, :]
    return jnp.max(jnp.where(matches, doc_of_block[None, :], -1), axis=1)


def update(state_now, query_head_rows, key_piece, value_piece, visible):
    running_max, summed, totals = state_now
    rows_here = key_piece.shape[0]
    kv_heads = query_head_rows.shape[1]
    key_head_rows = key_piece.reshape(rows_here, kv_heads, HEAD_SIZE)
    value_head_rows = value_piece.reshape(rows_here, kv_heads, HEAD_SIZE)
    score_scale = 1.0 / math.sqrt(HEAD_SIZE)
    scores = (
        jnp.einsum(
            "qhgd,khd->hgqk", query_head_rows, key_head_rows, preferred_element_type=jnp.float32
        )
        * score_scale
    )
    scores = jnp.where(visible, scores, -1e30)
    new_max = jnp.maximum(running_max, jnp.max(scores, axis=-1))
    weights = jnp.where(visible, jnp.exp(scores - new_max[..., None]), 0.0)
    rescale = jnp.exp(running_max - new_max)
    products = jnp.einsum(
        "hgqk,khd->hgqd",
        weights.astype(jnp.bfloat16),
        value_head_rows,
        preferred_element_type=jnp.float32,
    )
    summed = summed * rescale[..., None] + products
    totals = totals * rescale + jnp.sum(weights, axis=-1)
    return (new_max, summed, totals)


def fresh_state(kv_heads, group_width, rows_here):
    return (
        jnp.full((kv_heads, group_width, rows_here), -1e30, jnp.float32),
        jnp.zeros((kv_heads, group_width, rows_here, HEAD_SIZE), jnp.float32),
        jnp.zeros((kv_heads, group_width, rows_here), jnp.float32),
    )


def finish(state_now, rows_here, q_heads):
    running_max, summed, totals = state_now
    attended = summed / totals[..., None]
    return (
        jnp.transpose(attended, (2, 0, 1, 3))
        .reshape(rows_here, q_heads * HEAD_SIZE)
        .astype(jnp.bfloat16)
    )


def head_features(attended):
    head_count = lax.axis_size("head")
    head_index = lax.axis_index("head")
    received = [attended]
    for shift in range(1, head_count):
        pairs = [(i, (i + shift) % head_count) for i in range(head_count)]
        received.append(lax.ppermute(attended, "head", pairs))
    pieces = []
    for source in range(head_count):
        shift_of = (head_index + head_count - source) % head_count
        piece = received[0]
        for shift in range(1, head_count):
            piece = jnp.where(shift_of == shift, received[shift], piece)
        pieces.append(piece)
    return jnp.concatenate(pieces, axis=1)


def ring_transfer(out_weight):
    count = lax.axis_size("ctx")
    order = list(range(0, count, 2)) + sorted(range(1, count, 2), reverse=True)
    position_of = [0] * count
    for position, index in enumerate(order):
        position_of[index] = position
    ctx_index = lax.axis_index("ctx")
    position = jnp.asarray(position_of, jnp.int32)[ctx_index]
    order_table = jnp.asarray(order, jnp.int32)
    columns = out_weight.shape[1]
    groups = lax.axis_size("group")
    group_index = lax.axis_index("group")
    own = (columns // 4) // 128 * 128 if groups == 2 else 0
    shared = columns - groups * own if own else columns
    swap = [(0, 1), (1, 0)]

    def carried(block):
        if not own:
            return block
        mine = lax.dynamic_slice_in_dim(block, shared + group_index * own, own, 1)
        return jnp.concatenate([block[:, :shared], mine], axis=1)

    def other_of(block):
        return lax.dynamic_slice_in_dim(block, shared + (1 - group_index) * own, own, 1)

    arrivals = [(ctx_index, carried(out_weight), other_of(out_weight) if own else None)]
    ahead = [(order[p], order[(p + 1) % count]) for p in range(count)]
    behind = [(order[p], order[(p - 1) % count]) for p in range(count)]
    forward = backward = carried(out_weight)
    forward_steps = count // 2
    backward_steps = count - 1 - forward_steps
    for step in range(1, forward_steps + 1):
        forward = lax.ppermute(forward, "ctx", ahead)
        crossed = lax.ppermute(forward[:, shared:], "group", swap) if own else None
        arrivals.append((order_table[(position + count - step) % count], forward, crossed))
        if step <= backward_steps:
            backward = lax.ppermute(backward, "ctx", behind)
            crossed = lax.ppermute(backward[:, shared:], "group", swap) if own else None
            arrivals.append((order_table[(position + step) % count], backward, crossed))
    return arrivals, shared, own


def ring_project(features, arrivals, shared, own, rows):
    group_index = lax.axis_index("group")
    parts = None
    for source, carried_block, crossed in arrivals:
        piece = lax.dynamic_slice_in_dim(features, source * rows, rows, 1)
        terms = [jnp.dot(piece, carried_block, preferred_element_type=jnp.float32)]
        if own:
            terms.append(jnp.dot(piece, crossed, preferred_element_type=jnp.float32))
        parts = terms if parts is None else [a + b for a, b in zip(parts, terms)]
    if not own:
        return parts[0]
    mine, other = parts[0][:, shared:], parts[1]
    first = jnp.where(group_index == 0, mine, other)
    second = jnp.where(group_index == 0, other, mine)
    return jnp.concatenate([parts[0][:, :shared], first, second], axis=1)

def per_device(queries, keys, values, doc_of_block, out_weight):
    tok_rows = queries.shape[0]
    kv_heads = keys.shape[1] // HEAD_SIZE
    q_heads = queries.shape[1] // HEAD_SIZE
    group_width = q_heads // kv_heads
    ctx_count = lax.axis_size("ctx")
    reach_devs = min(8, ctx_count // 2)
    ctx_index = lax.axis_index("ctx")
    query_start = ctx_index * tok_rows
    query_pos = query_start + jnp.arange(tok_rows, dtype=jnp.int32)
    query_doc = lookup_docs(query_pos, doc_of_block)
    query_head_rows = queries.reshape(tok_rows, kv_heads, group_width, HEAD_SIZE)

    def attend(state_now, key_piece, value_piece, key_start):
        key_pos = key_start + jnp.arange(key_piece.shape[0], dtype=jnp.int32)
        key_doc = lookup_docs(key_pos, doc_of_block)
        visible = (key_doc[None, :] == query_doc[:, None]) & (
            key_pos[None, :] <= query_pos[:, None]
        )
        return update(state_now, query_head_rows, key_piece, value_piece, visible)

    arrivals, shared, own = ring_transfer(out_weight)
    initial_state = fresh_state(kv_heads, group_width, tok_rows)
    state_now = attend(initial_state, keys, values, query_start)
    joined = jnp.concatenate([keys, values], axis=1)
    for distance in range(1, reach_devs + 1):
        skipped = BLOCK_TOKENS if distance == reach_devs and tok_rows > BLOCK_TOKENS else 0
        prior = passed_along(joined[skipped:], "ctx", distance)
        prior_keys, prior_values = prior[:, : keys.shape[1]], prior[:, keys.shape[1] :]
        key_start = query_start - distance * tok_rows + skipped
        state_now = attend(state_now, prior_keys, prior_values, key_start)
    attended = finish(state_now, tok_rows, q_heads)
    features = head_features(attended)
    mixed = ring_project(features, arrivals, shared, own, out_weight.shape[0])
    return mixed.astype(jnp.bfloat16)


def solution(mesh):
    return jax.shard_map(
        per_device,
        mesh=mesh,
        in_specs=(
            P(("group", "ctx"), "head"),
            P(("group", "ctx"), "head"),
            P(("group", "ctx"), "head"),
            P("group"),
            P("ctx", "head"),
        ),
        out_specs=P(("group", "ctx"), "head"),
        check_vma=False,
    )
```

```python
import math

import jax
import jax.numpy as jnp
from jax import lax
from jax.sharding import PartitionSpec as P

HEAD_SIZE = 128
BLOCK_TOKENS = 128


def passed_along(array, axis, by):
    peers = lax.axis_size(axis)
    pairs = [(i, i + by) for i in range(peers) if 0 <= i + by < peers]
    return lax.ppermute(array, axis, pairs)


def lookup_docs(positions, doc_of_block):
    block_ids = jnp.floor_divide(positions, BLOCK_TOKENS)
    table_ids = jnp.arange(doc_of_block.shape[0], dtype=jnp.int32)
    matches = block_ids[:, None] == table_ids[None, :]
    return jnp.max(jnp.where(matches, doc_of_block[None, :], -1), axis=1)


def update(state_now, query_head_rows, key_piece, value_piece, visible):
    running_max, summed, totals = state_now
    rows_here = key_piece.shape[0]
    kv_heads = query_head_rows.shape[1]
    key_head_rows = key_piece.reshape(rows_here, kv_heads, HEAD_SIZE)
    value_head_rows = value_piece.reshape(rows_here, kv_heads, HEAD_SIZE)
    score_scale = 1.0 / math.sqrt(HEAD_SIZE)
    scores = (
        jnp.einsum(
            "qhgd,khd->hgqk", query_head_rows, key_head_rows, preferred_element_type=jnp.float32
        )
        * score_scale
    )
    scores = jnp.where(visible, scores, -1e30)
    new_max = jnp.maximum(running_max, jnp.max(scores, axis=-1))
    weights = jnp.where(visible, jnp.exp(scores - new_max[..., None]), 0.0)
    rescale = jnp.exp(running_max - new_max)
    products = jnp.einsum(
        "hgqk,khd->hgqd",
        weights.astype(jnp.bfloat16),
        value_head_rows,
        preferred_element_type=jnp.float32,
    )
    summed = summed * rescale[..., None] + products
    totals = totals * rescale + jnp.sum(weights, axis=-1)
    return (new_max, summed, totals)


def fresh_state(kv_heads, group_width, rows_here):
    return (
        jnp.full((kv_heads, group_width, rows_here), -1e30, jnp.float32),
        jnp.zeros((kv_heads, group_width, rows_here, HEAD_SIZE), jnp.float32),
        jnp.zeros((kv_heads, group_width, rows_here), jnp.float32),
    )


def finish(state_now, rows_here, q_heads):
    running_max, summed, totals = state_now
    attended = summed / totals[..., None]
    return (
        jnp.transpose(attended, (2, 0, 1, 3))
        .reshape(rows_here, q_heads * HEAD_SIZE)
        .astype(jnp.bfloat16)
    )


def head_features(attended):
    head_count = lax.axis_size("head")
    head_index = lax.axis_index("head")
    received = [attended]
    for shift in range(1, head_count):
        pairs = [(i, (i + shift) % head_count) for i in range(head_count)]
        received.append(lax.ppermute(attended, "head", pairs))
    pieces = []
    for source in range(head_count):
        shift_of = (head_index + head_count - source) % head_count
        piece = received[0]
        for shift in range(1, head_count):
            piece = jnp.where(shift_of == shift, received[shift], piece)
        pieces.append(piece)
    return jnp.concatenate(pieces, axis=1)


def ring_transfer(out_weight):
    count = lax.axis_size("ctx")
    order = list(range(0, count, 2)) + sorted(range(1, count, 2), reverse=True)
    position_of = [0] * count
    for position, index in enumerate(order):
        position_of[index] = position
    ctx_index = lax.axis_index("ctx")
    position = jnp.asarray(position_of, jnp.int32)[ctx_index]
    order_table = jnp.asarray(order, jnp.int32)
    columns = out_weight.shape[1]
    groups = lax.axis_size("group")
    group_index = lax.axis_index("group")
    own = (columns // 3) // 128 * 128 if groups == 2 else 0
    shared = columns - groups * own if own else columns
    swap = [(0, 1), (1, 0)]

    def carried(block):
        if not own:
            return block
        mine = lax.dynamic_slice_in_dim(block, shared + group_index * own, own, 1)
        return jnp.concatenate([block[:, :shared], mine], axis=1)

    def other_of(block):
        return lax.dynamic_slice_in_dim(block, shared + (1 - group_index) * own, own, 1)

    arrivals = [(ctx_index, carried(out_weight), other_of(out_weight) if own else None)]
    ahead = [(order[p], order[(p + 1) % count]) for p in range(count)]
    behind = [(order[p], order[(p - 1) % count]) for p in range(count)]
    forward = backward = carried(out_weight)
    forward_steps = count // 2
    backward_steps = count - 1 - forward_steps
    for step in range(1, forward_steps + 1):
        forward = lax.ppermute(forward, "ctx", ahead)
        crossed = lax.ppermute(forward[:, shared:], "group", swap) if own else None
        arrivals.append((order_table[(position + count - step) % count], forward, crossed))
        if step <= backward_steps:
            backward = lax.ppermute(backward, "ctx", behind)
            crossed = lax.ppermute(backward[:, shared:], "group", swap) if own else None
            arrivals.append((order_table[(position + step) % count], backward, crossed))
    return arrivals, shared, own


def ring_project(features, arrivals, shared, own, rows):
    group_index = lax.axis_index("group")
    parts = None
    for source, carried_block, crossed in arrivals:
        piece = lax.dynamic_slice_in_dim(features, source * rows, rows, 1)
        terms = [jnp.dot(piece, carried_block, preferred_element_type=jnp.float32)]
        if own:
            terms.append(jnp.dot(piece, crossed, preferred_element_type=jnp.float32))
        parts = terms if parts is None else [a + b for a, b in zip(parts, terms)]
    if not own:
        return parts[0]
    mine, other = parts[0][:, shared:], parts[1]
    first = jnp.where(group_index == 0, mine, other)
    second = jnp.where(group_index == 0, other, mine)
    return jnp.concatenate([parts[0][:, :shared], first, second], axis=1)

def per_device(queries, keys, values, doc_of_block, out_weight):
    tok_rows = queries.shape[0]
    kv_heads = keys.shape[1] // HEAD_SIZE
    q_heads = queries.shape[1] // HEAD_SIZE
    group_width = q_heads // kv_heads
    ctx_count = lax.axis_size("ctx")
    reach_devs = min(8, ctx_count // 2)
    ctx_index = lax.axis_index("ctx")
    query_start = ctx_index * tok_rows
    query_pos = query_start + jnp.arange(tok_rows, dtype=jnp.int32)
    query_doc = lookup_docs(query_pos, doc_of_block)
    query_head_rows = queries.reshape(tok_rows, kv_heads, group_width, HEAD_SIZE)

    def attend(state_now, key_piece, value_piece, key_start):
        key_pos = key_start + jnp.arange(key_piece.shape[0], dtype=jnp.int32)
        key_doc = lookup_docs(key_pos, doc_of_block)
        visible = (key_doc[None, :] == query_doc[:, None]) & (
            key_pos[None, :] <= query_pos[:, None]
        )
        return update(state_now, query_head_rows, key_piece, value_piece, visible)

    arrivals, shared, own = ring_transfer(out_weight)
    initial_state = fresh_state(kv_heads, group_width, tok_rows)
    state_now = attend(initial_state, keys, values, query_start)
    joined = jnp.concatenate([keys, values], axis=1)
    for distance in range(1, reach_devs + 1):
        skipped = BLOCK_TOKENS if distance == reach_devs and tok_rows > BLOCK_TOKENS else 0
        prior = passed_along(joined[skipped:], "ctx", distance)
        prior_keys, prior_values = prior[:, : keys.shape[1]], prior[:, keys.shape[1] :]
        key_start = query_start - distance * tok_rows + skipped
        state_now = attend(state_now, prior_keys, prior_values, key_start)
    attended = finish(state_now, tok_rows, q_heads)
    features = head_features(attended)
    mixed = ring_project(features, arrivals, shared, own, out_weight.shape[0])
    return mixed.astype(jnp.bfloat16)


def solution(mesh):
    return jax.shard_map(
        per_device,
        mesh=mesh,
        in_specs=(
            P(("group", "ctx"), "head"),
            P(("group", "ctx"), "head"),
            P(("group", "ctx"), "head"),
            P("group"),
            P("ctx", "head"),
        ),
        out_specs=P(("group", "ctx"), "head"),
        check_vma=False,
    )
```

```python
import math

import jax
import jax.numpy as jnp
from jax import lax
from jax.sharding import PartitionSpec as P

HEAD_SIZE = 128
BLOCK_TOKENS = 128


def passed_along(array, axis, by):
    peers = lax.axis_size(axis)
    pairs = [(i, i + by) for i in range(peers) if 0 <= i + by < peers]
    return lax.ppermute(array, axis, pairs)


def lookup_docs(positions, doc_of_block):
    block_ids = jnp.floor_divide(positions, BLOCK_TOKENS)
    table_ids = jnp.arange(doc_of_block.shape[0], dtype=jnp.int32)
    matches = block_ids[:, None] == table_ids[None, :]
    return jnp.max(jnp.where(matches, doc_of_block[None, :], -1), axis=1)


def update(state_now, query_head_rows, key_piece, value_piece, visible):
    running_max, summed, totals = state_now
    rows_here = key_piece.shape[0]
    kv_heads = query_head_rows.shape[1]
    key_head_rows = key_piece.reshape(rows_here, kv_heads, HEAD_SIZE)
    value_head_rows = value_piece.reshape(rows_here, kv_heads, HEAD_SIZE)
    score_scale = 1.0 / math.sqrt(HEAD_SIZE)
    scores = (
        jnp.einsum(
            "qhgd,khd->hgqk", query_head_rows, key_head_rows, preferred_element_type=jnp.float32
        )
        * score_scale
    )
    scores = jnp.where(visible, scores, -1e30)
    new_max = jnp.maximum(running_max, jnp.max(scores, axis=-1))
    weights = jnp.where(visible, jnp.exp(scores - new_max[..., None]), 0.0)
    rescale = jnp.exp(running_max - new_max)
    products = jnp.einsum(
        "hgqk,khd->hgqd",
        weights.astype(jnp.bfloat16),
        value_head_rows,
        preferred_element_type=jnp.float32,
    )
    summed = summed * rescale[..., None] + products
    totals = totals * rescale + jnp.sum(weights, axis=-1)
    return (new_max, summed, totals)


def fresh_state(kv_heads, group_width, rows_here):
    return (
        jnp.full((kv_heads, group_width, rows_here), -1e30, jnp.float32),
        jnp.zeros((kv_heads, group_width, rows_here, HEAD_SIZE), jnp.float32),
        jnp.zeros((kv_heads, group_width, rows_here), jnp.float32),
    )


def finish(state_now, rows_here, q_heads):
    running_max, summed, totals = state_now
    attended = summed / totals[..., None]
    return (
        jnp.transpose(attended, (2, 0, 1, 3))
        .reshape(rows_here, q_heads * HEAD_SIZE)
        .astype(jnp.bfloat16)
    )


def head_features(attended):
    head_count = lax.axis_size("head")
    head_index = lax.axis_index("head")
    received = [attended]
    for shift in range(1, head_count):
        pairs = [(i, (i + shift) % head_count) for i in range(head_count)]
        received.append(lax.ppermute(attended, "head", pairs))
    pieces = []
    for source in range(head_count):
        shift_of = (head_index + head_count - source) % head_count
        piece = received[0]
        for shift in range(1, head_count):
            piece = jnp.where(shift_of == shift, received[shift], piece)
        pieces.append(piece)
    return jnp.concatenate(pieces, axis=1)


def ring_transfer(out_weight):
    count = lax.axis_size("ctx")
    order = list(range(0, count, 2)) + sorted(range(1, count, 2), reverse=True)
    position_of = [0] * count
    for position, index in enumerate(order):
        position_of[index] = position
    ctx_index = lax.axis_index("ctx")
    position = jnp.asarray(position_of, jnp.int32)[ctx_index]
    order_table = jnp.asarray(order, jnp.int32)
    columns = out_weight.shape[1]
    groups = lax.axis_size("group")
    group_index = lax.axis_index("group")
    own = (columns // 4) // 128 * 128 if groups == 2 else 0
    shared = columns - groups * own if own else columns
    swap = [(0, 1), (1, 0)]

    def carried(block):
        if not own:
            return block
        mine = lax.dynamic_slice_in_dim(block, shared + group_index * own, own, 1)
        return jnp.concatenate([block[:, :shared], mine], axis=1)

    def other_of(block):
        return lax.dynamic_slice_in_dim(block, shared + (1 - group_index) * own, own, 1)

    arrivals = [(ctx_index, carried(out_weight), other_of(out_weight) if own else None)]
    ahead = [(order[p], order[(p + 1) % count]) for p in range(count)]
    behind = [(order[p], order[(p - 1) % count]) for p in range(count)]
    forward = backward = carried(out_weight)
    forward_steps = count // 2
    backward_steps = count - 1 - forward_steps
    for step in range(1, forward_steps + 1):
        forward = lax.ppermute(forward, "ctx", ahead)
        crossed = lax.ppermute(forward[:, shared:], "group", swap) if own else None
        arrivals.append((order_table[(position + count - step) % count], forward, crossed))
        if step <= backward_steps:
            backward = lax.ppermute(backward, "ctx", behind)
            crossed = lax.ppermute(backward[:, shared:], "group", swap) if own else None
            arrivals.append((order_table[(position + step) % count], backward, crossed))
    return arrivals, shared, own


def ring_project(features, arrivals, shared, own, rows):
    group_index = lax.axis_index("group")
    parts = None
    for source, carried_block, crossed in arrivals:
        piece = lax.dynamic_slice_in_dim(features, source * rows, rows, 1)
        terms = [jnp.dot(piece, carried_block, preferred_element_type=jnp.float32)]
        if own:
            terms.append(jnp.dot(piece, crossed, preferred_element_type=jnp.float32))
        parts = terms if parts is None else [a + b for a, b in zip(parts, terms)]
    if not own:
        return parts[0]
    mine, other = parts[0][:, shared:], parts[1]
    first = jnp.where(group_index == 0, mine, other)
    second = jnp.where(group_index == 0, other, mine)
    return jnp.concatenate([parts[0][:, :shared], first, second], axis=1)

def per_device(queries, keys, values, doc_of_block, out_weight):
    tok_rows = queries.shape[0]
    kv_heads = keys.shape[1] // HEAD_SIZE
    q_heads = queries.shape[1] // HEAD_SIZE
    group_width = q_heads // kv_heads
    ctx_count = lax.axis_size("ctx")
    reach_devs = min(8, ctx_count // 2)
    ctx_index = lax.axis_index("ctx")
    query_start = ctx_index * tok_rows
    query_pos = query_start + jnp.arange(tok_rows, dtype=jnp.int32)
    query_doc = lookup_docs(query_pos, doc_of_block)
    query_head_rows = queries.reshape(tok_rows, kv_heads, group_width, HEAD_SIZE)

    def attend(state_now, key_piece, value_piece, key_start):
        key_pos = key_start + jnp.arange(key_piece.shape[0], dtype=jnp.int32)
        key_doc = lookup_docs(key_pos, doc_of_block)
        visible = (key_doc[None, :] == query_doc[:, None]) & (
            key_pos[None, :] <= query_pos[:, None]
        )
        return update(state_now, query_head_rows, key_piece, value_piece, visible)

    arrivals, shared, own = ring_transfer(out_weight)
    initial_state = fresh_state(kv_heads, group_width, tok_rows)
    state_now = attend(initial_state, keys, values, query_start)
    joined = jnp.concatenate([keys, values], axis=1)
    for distance in range(1, reach_devs + 1):
        skipped = BLOCK_TOKENS if distance == reach_devs and tok_rows > BLOCK_TOKENS else 0
        prior = passed_along(joined[skipped:], "ctx", distance)
        prior_keys, prior_values = prior[:, : keys.shape[1]], prior[:, keys.shape[1] :]
        key_start = query_start - distance * tok_rows + skipped
        state_now = attend(state_now, prior_keys, prior_values, key_start)
    attended = finish(state_now, tok_rows, q_heads)
    first = [index for index in (1, 2) if index < len(arrivals) and arrivals[index][2] is not None]
    attended, crossed = lax.optimization_barrier((attended, [arrivals[i][2] for i in first]))
    for index, value in zip(first, crossed):
        arrivals[index] = (arrivals[index][0], arrivals[index][1], value)
    features = head_features(attended)
    mixed = ring_project(features, arrivals, shared, own, out_weight.shape[0])
    return mixed.astype(jnp.bfloat16)


def solution(mesh):
    return jax.shard_map(
        per_device,
        mesh=mesh,
        in_specs=(
            P(("group", "ctx"), "head"),
            P(("group", "ctx"), "head"),
            P(("group", "ctx"), "head"),
            P("group"),
            P("ctx", "head"),
        ),
        out_specs=P(("group", "ctx"), "head"),
        check_vma=False,
    )
```

```python
import math

import jax
import jax.numpy as jnp
from jax import lax
from jax.sharding import PartitionSpec as P

HEAD_SIZE = 128
BLOCK_TOKENS = 128


def passed_along(array, axis, by):
    peers = lax.axis_size(axis)
    pairs = [(i, i + by) for i in range(peers) if 0 <= i + by < peers]
    return lax.ppermute(array, axis, pairs)


def lookup_docs(positions, doc_of_block):
    block_ids = jnp.floor_divide(positions, BLOCK_TOKENS)
    table_ids = jnp.arange(doc_of_block.shape[0], dtype=jnp.int32)
    matches = block_ids[:, None] == table_ids[None, :]
    return jnp.max(jnp.where(matches, doc_of_block[None, :], -1), axis=1)


def update(state_now, query_head_rows, key_piece, value_piece, visible):
    running_max, summed, totals = state_now
    rows_here = key_piece.shape[0]
    kv_heads = query_head_rows.shape[1]
    key_head_rows = key_piece.reshape(rows_here, kv_heads, HEAD_SIZE)
    value_head_rows = value_piece.reshape(rows_here, kv_heads, HEAD_SIZE)
    score_scale = 1.0 / math.sqrt(HEAD_SIZE)
    scores = (
        jnp.einsum(
            "qhgd,khd->hgqk", query_head_rows, key_head_rows, preferred_element_type=jnp.float32
        )
        * score_scale
    )
    scores = jnp.where(visible, scores, -1e30)
    new_max = jnp.maximum(running_max, jnp.max(scores, axis=-1))
    weights = jnp.where(visible, jnp.exp(scores - new_max[..., None]), 0.0)
    rescale = jnp.exp(running_max - new_max)
    products = jnp.einsum(
        "hgqk,khd->hgqd",
        weights.astype(jnp.bfloat16),
        value_head_rows,
        preferred_element_type=jnp.float32,
    )
    summed = summed * rescale[..., None] + products
    totals = totals * rescale + jnp.sum(weights, axis=-1)
    return (new_max, summed, totals)


def fresh_state(kv_heads, group_width, rows_here):
    return (
        jnp.full((kv_heads, group_width, rows_here), -1e30, jnp.float32),
        jnp.zeros((kv_heads, group_width, rows_here, HEAD_SIZE), jnp.float32),
        jnp.zeros((kv_heads, group_width, rows_here), jnp.float32),
    )


def finish(state_now, rows_here, q_heads):
    running_max, summed, totals = state_now
    attended = summed / totals[..., None]
    return (
        jnp.transpose(attended, (2, 0, 1, 3))
        .reshape(rows_here, q_heads * HEAD_SIZE)
        .astype(jnp.bfloat16)
    )


def head_features(attended):
    head_count = lax.axis_size("head")
    head_index = lax.axis_index("head")
    received = [attended]
    for shift in range(1, head_count):
        pairs = [(i, (i + shift) % head_count) for i in range(head_count)]
        received.append(lax.ppermute(attended, "head", pairs))
    pieces = []
    for source in range(head_count):
        shift_of = (head_index + head_count - source) % head_count
        piece = received[0]
        for shift in range(1, head_count):
            piece = jnp.where(shift_of == shift, received[shift], piece)
        pieces.append(piece)
    return jnp.concatenate(pieces, axis=1)


def ring_transfer(out_weight):
    count = lax.axis_size("ctx")
    order = list(range(0, count, 2)) + sorted(range(1, count, 2), reverse=True)
    position_of = [0] * count
    for position, index in enumerate(order):
        position_of[index] = position
    ctx_index = lax.axis_index("ctx")
    position = jnp.asarray(position_of, jnp.int32)[ctx_index]
    order_table = jnp.asarray(order, jnp.int32)
    columns = out_weight.shape[1]
    groups = lax.axis_size("group")
    group_index = lax.axis_index("group")
    own = (columns // 4) // 128 * 128 if groups == 2 else 0
    shared = columns - groups * own if own else columns
    swap = [(0, 1), (1, 0)]

    def carried(block):
        if not own:
            return block
        mine = lax.dynamic_slice_in_dim(block, shared + group_index * own, own, 1)
        return jnp.concatenate([block[:, :shared], mine], axis=1)

    def other_of(block):
        return lax.dynamic_slice_in_dim(block, shared + (1 - group_index) * own, own, 1)

    arrivals = [(ctx_index, carried(out_weight), other_of(out_weight) if own else None)]
    ahead = [(order[p], order[(p + 1) % count]) for p in range(count)]
    behind = [(order[p], order[(p - 1) % count]) for p in range(count)]
    forward = backward = carried(out_weight)
    forward_steps = count // 2
    backward_steps = count - 1 - forward_steps
    for step in range(1, forward_steps + 1):
        forward = lax.ppermute(forward, "ctx", ahead)
        if step > backward_steps:
            crossed = lax.ppermute(forward[:, shared:], "group", swap) if own else None
            arrivals.append((order_table[(position + count - step) % count], forward, crossed))
            continue
        backward = lax.ppermute(backward, "ctx", behind)
        both = None
        if own:
            both = lax.ppermute(
                jnp.concatenate([forward[:, shared:], backward[:, shared:]], axis=0), "group", swap
            )
        rows = forward.shape[0]
        arrivals.append(
            (order_table[(position + count - step) % count], forward, both[:rows] if own else None)
        )
        arrivals.append((order_table[(position + step) % count], backward, both[rows:] if own else None))
    return arrivals, shared, own


def ring_project(features, arrivals, shared, own, rows):
    group_index = lax.axis_index("group")
    parts = None
    for source, carried_block, crossed in arrivals:
        piece = lax.dynamic_slice_in_dim(features, source * rows, rows, 1)
        terms = [jnp.dot(piece, carried_block, preferred_element_type=jnp.float32)]
        if own:
            terms.append(jnp.dot(piece, crossed, preferred_element_type=jnp.float32))
        parts = terms if parts is None else [a + b for a, b in zip(parts, terms)]
    if not own:
        return parts[0]
    mine, other = parts[0][:, shared:], parts[1]
    first = jnp.where(group_index == 0, mine, other)
    second = jnp.where(group_index == 0, other, mine)
    return jnp.concatenate([parts[0][:, :shared], first, second], axis=1)

def per_device(queries, keys, values, doc_of_block, out_weight):
    tok_rows = queries.shape[0]
    kv_heads = keys.shape[1] // HEAD_SIZE
    q_heads = queries.shape[1] // HEAD_SIZE
    group_width = q_heads // kv_heads
    ctx_count = lax.axis_size("ctx")
    reach_devs = min(8, ctx_count // 2)
    ctx_index = lax.axis_index("ctx")
    query_start = ctx_index * tok_rows
    query_pos = query_start + jnp.arange(tok_rows, dtype=jnp.int32)
    query_doc = lookup_docs(query_pos, doc_of_block)
    query_head_rows = queries.reshape(tok_rows, kv_heads, group_width, HEAD_SIZE)

    def attend(state_now, key_piece, value_piece, key_start):
        key_pos = key_start + jnp.arange(key_piece.shape[0], dtype=jnp.int32)
        key_doc = lookup_docs(key_pos, doc_of_block)
        visible = (key_doc[None, :] == query_doc[:, None]) & (
            key_pos[None, :] <= query_pos[:, None]
        )
        return update(state_now, query_head_rows, key_piece, value_piece, visible)

    arrivals, shared, own = ring_transfer(out_weight)
    initial_state = fresh_state(kv_heads, group_width, tok_rows)
    state_now = attend(initial_state, keys, values, query_start)
    joined = jnp.concatenate([keys, values], axis=1)
    for distance in range(1, reach_devs + 1):
        skipped = BLOCK_TOKENS if distance == reach_devs and tok_rows > BLOCK_TOKENS else 0
        prior = passed_along(joined[skipped:], "ctx", distance)
        prior_keys, prior_values = prior[:, : keys.shape[1]], prior[:, keys.shape[1] :]
        key_start = query_start - distance * tok_rows + skipped
        state_now = attend(state_now, prior_keys, prior_values, key_start)
    attended = finish(state_now, tok_rows, q_heads)
    features = head_features(attended)
    mixed = ring_project(features, arrivals, shared, own, out_weight.shape[0])
    return mixed.astype(jnp.bfloat16)


def solution(mesh):
    return jax.shard_map(
        per_device,
        mesh=mesh,
        in_specs=(
            P(("group", "ctx"), "head"),
            P(("group", "ctx"), "head"),
            P(("group", "ctx"), "head"),
            P("group"),
            P("ctx", "head"),
        ),
        out_specs=P(("group", "ctx"), "head"),
        check_vma=False,
    )
```

```python
import math

import jax
import jax.numpy as jnp
from jax import lax
from jax.sharding import PartitionSpec as P

HEAD_SIZE = 128
BLOCK_TOKENS = 128


def passed_along(array, axis, by):
    peers = lax.axis_size(axis)
    pairs = [(i, i + by) for i in range(peers) if 0 <= i + by < peers]
    return lax.ppermute(array, axis, pairs)


def lookup_docs(positions, doc_of_block):
    block_ids = jnp.floor_divide(positions, BLOCK_TOKENS)
    table_ids = jnp.arange(doc_of_block.shape[0], dtype=jnp.int32)
    matches = block_ids[:, None] == table_ids[None, :]
    return jnp.max(jnp.where(matches, doc_of_block[None, :], -1), axis=1)


def update(state_now, query_head_rows, key_piece, value_piece, visible):
    running_max, summed, totals = state_now
    rows_here = key_piece.shape[0]
    kv_heads = query_head_rows.shape[1]
    key_head_rows = key_piece.reshape(rows_here, kv_heads, HEAD_SIZE)
    value_head_rows = value_piece.reshape(rows_here, kv_heads, HEAD_SIZE)
    score_scale = 1.0 / math.sqrt(HEAD_SIZE)
    scores = (
        jnp.einsum(
            "qhgd,khd->hgqk", query_head_rows, key_head_rows, preferred_element_type=jnp.float32
        )
        * score_scale
    )
    scores = jnp.where(visible, scores, -1e30)
    new_max = jnp.maximum(running_max, jnp.max(scores, axis=-1))
    weights = jnp.where(visible, jnp.exp(scores - new_max[..., None]), 0.0)
    rescale = jnp.exp(running_max - new_max)
    products = jnp.einsum(
        "hgqk,khd->hgqd",
        weights.astype(jnp.bfloat16),
        value_head_rows,
        preferred_element_type=jnp.float32,
    )
    summed = summed * rescale[..., None] + products
    totals = totals * rescale + jnp.sum(weights, axis=-1)
    return (new_max, summed, totals)


def fresh_state(kv_heads, group_width, rows_here):
    return (
        jnp.full((kv_heads, group_width, rows_here), -1e30, jnp.float32),
        jnp.zeros((kv_heads, group_width, rows_here, HEAD_SIZE), jnp.float32),
        jnp.zeros((kv_heads, group_width, rows_here), jnp.float32),
    )


def finish(state_now, rows_here, q_heads):
    running_max, summed, totals = state_now
    attended = summed / totals[..., None]
    return (
        jnp.transpose(attended, (2, 0, 1, 3))
        .reshape(rows_here, q_heads * HEAD_SIZE)
        .astype(jnp.bfloat16)
    )


def head_features(attended):
    head_count = lax.axis_size("head")
    head_index = lax.axis_index("head")
    received = [attended]
    for shift in range(1, head_count):
        pairs = [(i, (i + shift) % head_count) for i in range(head_count)]
        received.append(lax.ppermute(attended, "head", pairs))
    pieces = []
    for source in range(head_count):
        shift_of = (head_index + head_count - source) % head_count
        piece = received[0]
        for shift in range(1, head_count):
            piece = jnp.where(shift_of == shift, received[shift], piece)
        pieces.append(piece)
    return jnp.concatenate(pieces, axis=1)


def ring_transfer(out_weight):
    count = lax.axis_size("ctx")
    order = list(range(0, count, 2)) + sorted(range(1, count, 2), reverse=True)
    position_of = [0] * count
    for position, index in enumerate(order):
        position_of[index] = position
    ctx_index = lax.axis_index("ctx")
    position = jnp.asarray(position_of, jnp.int32)[ctx_index]
    order_table = jnp.asarray(order, jnp.int32)
    columns = out_weight.shape[1]
    groups = lax.axis_size("group")
    group_index = lax.axis_index("group")
    own = (columns // 4) // 128 * 128 if groups == 2 else 0
    shared = columns - groups * own if own else columns
    swap = [(0, 1), (1, 0)]

    def carried(block):
        if not own:
            return block
        mine = lax.dynamic_slice_in_dim(block, shared + group_index * own, own, 1)
        return jnp.concatenate([block[:, :shared], mine], axis=1)

    def other_of(block):
        return lax.dynamic_slice_in_dim(block, shared + (1 - group_index) * own, own, 1)

    arrivals = [(ctx_index, carried(out_weight), other_of(out_weight) if own else None)]
    ahead = [(order[p], order[(p + 1) % count]) for p in range(count)]
    behind = [(order[p], order[(p - 1) % count]) for p in range(count)]
    forward = backward = carried(out_weight)
    forward_steps = count // 2
    backward_steps = count - 1 - forward_steps
    for step in range(1, forward_steps + 1):
        forward = lax.ppermute(forward, "ctx", ahead)
        crossed = lax.ppermute(forward[:, shared:], "group", swap) if own else None
        arrivals.append((order_table[(position + count - step) % count], forward, crossed))
        if step <= backward_steps:
            backward = lax.ppermute(backward, "ctx", behind)
            crossed = lax.ppermute(backward[:, shared:], "group", swap) if own else None
            arrivals.append((order_table[(position + step) % count], backward, crossed))
    return arrivals, shared, own


def ring_project(features, arrivals, shared, own, rows):
    group_index = lax.axis_index("group")
    parts = None
    for source, carried_block, crossed in arrivals:
        piece = lax.dynamic_slice_in_dim(features, source * rows, rows, 1)
        terms = [jnp.dot(piece, carried_block, preferred_element_type=jnp.float32)]
        if own:
            terms.append(jnp.dot(piece, crossed, preferred_element_type=jnp.float32))
        parts = terms if parts is None else [a + b for a, b in zip(parts, terms)]
    if not own:
        return parts[0]
    full = jnp.concatenate([parts[0], parts[1]], axis=1)
    return lax.dynamic_update_slice_in_dim(
        lax.dynamic_update_slice_in_dim(full, parts[0][:, shared:], shared + group_index * own, 1),
        parts[1],
        shared + (1 - group_index) * own,
        1,
    )

def per_device(queries, keys, values, doc_of_block, out_weight):
    tok_rows = queries.shape[0]
    kv_heads = keys.shape[1] // HEAD_SIZE
    q_heads = queries.shape[1] // HEAD_SIZE
    group_width = q_heads // kv_heads
    ctx_count = lax.axis_size("ctx")
    reach_devs = min(8, ctx_count // 2)
    ctx_index = lax.axis_index("ctx")
    query_start = ctx_index * tok_rows
    query_pos = query_start + jnp.arange(tok_rows, dtype=jnp.int32)
    query_doc = lookup_docs(query_pos, doc_of_block)
    query_head_rows = queries.reshape(tok_rows, kv_heads, group_width, HEAD_SIZE)

    def attend(state_now, key_piece, value_piece, key_start):
        key_pos = key_start + jnp.arange(key_piece.shape[0], dtype=jnp.int32)
        key_doc = lookup_docs(key_pos, doc_of_block)
        visible = (key_doc[None, :] == query_doc[:, None]) & (
            key_pos[None, :] <= query_pos[:, None]
        )
        return update(state_now, query_head_rows, key_piece, value_piece, visible)

    arrivals, shared, own = ring_transfer(out_weight)
    initial_state = fresh_state(kv_heads, group_width, tok_rows)
    state_now = attend(initial_state, keys, values, query_start)
    joined = jnp.concatenate([keys, values], axis=1)
    for distance in range(1, reach_devs + 1):
        skipped = BLOCK_TOKENS if distance == reach_devs and tok_rows > BLOCK_TOKENS else 0
        prior = passed_along(joined[skipped:], "ctx", distance)
        prior_keys, prior_values = prior[:, : keys.shape[1]], prior[:, keys.shape[1] :]
        key_start = query_start - distance * tok_rows + skipped
        state_now = attend(state_now, prior_keys, prior_values, key_start)
    attended = finish(state_now, tok_rows, q_heads)
    features = head_features(attended)
    mixed = ring_project(features, arrivals, shared, own, out_weight.shape[0])
    return mixed.astype(jnp.bfloat16)


def solution(mesh):
    return jax.shard_map(
        per_device,
        mesh=mesh,
        in_specs=(
            P(("group", "ctx"), "head"),
            P(("group", "ctx"), "head"),
            P(("group", "ctx"), "head"),
            P("group"),
            P("ctx", "head"),
        ),
        out_specs=P(("group", "ctx"), "head"),
        check_vma=False,
    )
```
